32 devices in a mesh: chol: 4 (over z), orb: 8 (over y, x, core).
Axes of the slice: x: 2, y: 2, z: 4, core: 2. Of those that a mesh axis runs over, the one named last changes fastest.
Arguments:
- chol_vec: bfloat16 [16, 1536, 1536], P('chol', 'orb'), may hold values from -6 to 6
- env_weight: float32 [1536], P('orb'), may hold values from -5 to 5
- lno_coef: bfloat16 [8, 1024, 384], P('orb'), may hold values from -0.1875 to 0.1875
- domain: int32 [8, 1024], replicated, may hold values from 0 to 1535, as said below
- block_fill: int32 [8, 8], replicated, may hold values from 32 to 128, as said below
- lno_count: int32 [8], replicated, may hold values from 144 to 384
Outputs:
- rotated: bfloat16 [16, 8, 384, 384], P('chol', 'orb')
- dressing: bfloat16 [8, 384, 384], P('orb')
The draws below stay inside these ranges and needn't reach their ends.
Inputs may be any that keep to these rules, and one draw needn't show every extreme that they name: `domain`: for each fragment and each j < 8, slots j * 128 to (j + 1) * 128 - 1 hold distinct orbitals of the row block o * 192 to (o + 1) * 192 - 1 of a single o; the 8 groups of a fragment lie in distinct row blocks. `block_fill`: every fragment has one full group.
All inputs are finite; a program needn't handle non-finite values.
Results may differ from the reference program's by a relative error of at most 0.0064.
Values may be sent and summed in bfloat16 or wider, within the bound.
No kernel may reach another device: no remote copies, remote signals or barrier semaphores. Data moves between devices by JAX's collectives and lax.ppermute only.
A program may use at most 192 MiB of HBM per device.

```python
import math
import jax
import jax.numpy as jnp
from jax import lax

ORB_DEV = 192
CAP = 128
NBLK = 8
NLNO = 384
DMAX = 1024
NCHOL = 16
NORB = 1536
NFRAG = 8


def domain_layout(key):
    key_blocks, key_rows, key_counts, key_full = jax.random.split(key, 4)
    block_keys = jax.random.split(key_blocks, NFRAG)
    blocks = jax.vmap(lambda subkey: jax.random.permutation(subkey, NFRAG)[:NBLK])(block_keys)
    row_keys = jax.random.split(key_rows, NFRAG * NBLK)
    row_choice = jax.vmap(lambda subkey: jax.random.permutation(subkey, ORB_DEV)[:CAP])(row_keys)
    row_choice = row_choice.reshape(NFRAG, NBLK, CAP)
    orbital_ids = blocks[:, :, None] * ORB_DEV + row_choice
    counts = jax.random.randint(key_counts, (NFRAG, NBLK), CAP // 4, CAP + 1)
    full_group = jax.random.randint(key_full, (NFRAG, 1), 0, NBLK)
    counts = jnp.where(jnp.arange(NBLK)[None, :] == full_group, CAP, counts)
    return (orbital_ids.reshape(NFRAG, NBLK * CAP).astype(jnp.int32), counts.astype(jnp.int32))


def draw_domain(key, part):
    orbital_ids, counts = domain_layout(jax.random.fold_in(key, 11))
    return orbital_ids


def draw_block_fill(key, part):
    orbital_ids, counts = domain_layout(jax.random.fold_in(key, 11))
    return counts


def draw_lno_count(key, part):
    key_counts, key_full = jax.random.split(jax.random.fold_in(key, 23))
    counts = jax.random.randint(key_counts, (NFRAG,), NLNO * 3 // 8, NLNO + 1)
    full_frag = jax.random.randint(key_full, (), 0, NFRAG)
    counts = jnp.where(jnp.arange(NFRAG) == full_frag, NLNO, counts)
    return counts.astype(jnp.int32)


def steps_of(key, dims, shards, least, top_value):
    def one(position, blocks):
        draws = jax.random.uniform(jax.random.fold_in(jax.random.fold_in(key, 6), position), (blocks,), jnp.float32, least / len(shards), top_value / len(shards))
        return jnp.repeat(jnp.exp(draws), dims[position] // blocks).reshape((-1,) + (1,) * (len(dims) - position - 1))

    factor_of = one(*shards[0])
    for cut in shards[1:]:
        factor_of = factor_of * one(*cut)
    return factor_of


def centred(stream_key, extent, width, most, cuts=(), kind=jnp.bfloat16):
    drawn = width * jax.random.normal(stream_key, extent, jnp.float32)
    if cuts:
        drawn = drawn * steps_of(stream_key, extent, cuts, -0.22, 0.18)
    return jnp.clip(drawn, -most, most).astype(kind)


def setup_inputs(seed: int = 0) -> dict:
    arg_keys = jax.random.split(jax.random.key(seed), 7)
    return {
        "chol_vec": centred(arg_keys[0], (NCHOL, NORB, NORB), 1.0, 6.0, ((0, 4), (1, 8))),
        "env_weight": centred(arg_keys[1], (NORB,), 1.0, 5.0, ((0, 8),), jnp.float32),
        "lno_coef": centred(arg_keys[2], (NFRAG, DMAX, NLNO), DMAX ** -0.5, 0.1875, ((0, 8),)),
        "domain": draw_domain(jax.random.fold_in(arg_keys[6], 71), 0),
        "block_fill": draw_block_fill(jax.random.fold_in(arg_keys[6], 71), 0),
        "lno_count": draw_lno_count(jax.random.fold_in(arg_keys[6], 71), 0),
    }


def reference(chol_vec, env_weight, lno_coef, domain, block_fill, lno_count):
    slot_index = jnp.arange(DMAX, dtype=jnp.int32)
    slot_ok = (slot_index % CAP)[None, :] < jnp.repeat(block_fill, CAP, axis=1)
    column_ok = jnp.arange(NLNO, dtype=jnp.int32)[None, :] < lno_count[:, None]
    keep_mask = (slot_ok[:, :, None] & column_ok[:, None, :]).astype(jnp.bfloat16)
    masked = lno_coef * keep_mask
    norm_factor = 1.0 / math.sqrt(NCHOL * NORB)

    def per_fragment(inputs):
        orbitals, coef = inputs
        columns = jnp.take(chol_vec, orbitals, axis=2)
        half_rot = jnp.dot(columns.reshape(NCHOL * NORB, DMAX), coef, preferred_element_type=jnp.float32)
        half_rot = half_rot.astype(jnp.bfloat16).reshape(NCHOL, NORB, NLNO)
        domain_rows = jnp.take(half_rot, orbitals, axis=1).astype(jnp.float32)
        turned = jnp.einsum('dn,gdm->gnm', coef.astype(jnp.float32), domain_rows, precision=lax.Precision.HIGHEST)
        weighted = (half_rot.astype(jnp.float32) * env_weight[None, :, None]).astype(jnp.bfloat16)
        dressing_part = lax.dot_general(weighted.reshape(-1, NLNO), half_rot.reshape(-1, NLNO), (((0,), (0,)), ((), ())), preferred_element_type=jnp.float32)
        return (turned.astype(jnp.bfloat16), (dressing_part * norm_factor).astype(jnp.bfloat16))
    turned_all, dressing = lax.map(per_fragment, (domain, masked))
    rotated = jnp.transpose(turned_all, (1, 0, 2, 3))
    return (rotated, dressing)
```

```python
import math

import jax
import jax.numpy as jnp
from jax import lax
from jax.sharding import PartitionSpec as P


def per_device(chol_vec, env_weight, lno_coef, domain, block_fill, lno_count):
    chol_local, orb_rows, orb_total = chol_vec.shape
    frag_total, slot_total = domain.shape
    group_count = block_fill.shape[1]
    group_width = slot_total // group_count
    lno_width = lno_coef.shape[2]
    chol_size = lax.axis_size("chol")
    orb_size = lax.axis_size("orb")
    my_index = lax.axis_index("orb")
    norm_factor = 1.0 / math.sqrt(chol_local * chol_size * orb_total)

    slot_index = jnp.arange(slot_total, dtype=jnp.int32)
    slot_ok = (slot_index % group_width)[None, :] < jnp.repeat(block_fill, group_width, axis=1)
    column_ok = jnp.arange(lno_width, dtype=jnp.int32)[None, :] < lno_count[:, None]
    keep_mask = (slot_ok[:, :, None] & column_ok[:, None, :]).astype(jnp.bfloat16)

    weight_all = lax.all_gather(env_weight, "orb", axis=0, tiled=True)
    all_coef = lax.all_gather(lno_coef, "orb", axis=0, tiled=True)
    masked = all_coef * keep_mask

    chol_t = chol_vec.reshape(chol_local * orb_rows, orb_total).T
    picked = jnp.take(chol_t, domain, axis=0)
    half = jnp.einsum(
        "fsk,fsa->fka", picked, masked, preferred_element_type=jnp.float32
    ).astype(jnp.bfloat16)
    half = half.reshape(frag_total, chol_local, orb_rows, lno_width)

    received = lax.all_to_all(half, "orb", split_axis=0, concat_axis=0, tiled=True)

    with jax.named_scope("dressing"):
        weighted = (
            received.astype(jnp.float32)
            * weight_all.reshape(orb_size, 1, orb_rows, 1)
        ).astype(jnp.bfloat16)
        dressing_part = lax.dot_general(
            weighted.reshape(-1, lno_width),
            received.reshape(-1, lno_width),
            (((0,), (0,)), ((), ())),
            preferred_element_type=jnp.float32,
        )
        dressing = (lax.psum(dressing_part, "chol") * norm_factor).astype(jnp.bfloat16)

    with jax.named_scope("rotated"):
        own_orbitals = lax.dynamic_index_in_dim(domain, my_index, 0, keepdims=False)
        own_coef = lax.dynamic_index_in_dim(masked, my_index, 0, keepdims=False)
        block = own_orbitals // orb_rows
        local = own_orbitals % orb_rows
        chol_ids = jnp.arange(chol_local, dtype=jnp.int32)
        flat_rows = (block[None, :] * chol_local + chol_ids[:, None]) * orb_rows + local[None, :]
        domain_rows = jnp.take(received.reshape(-1, lno_width), flat_rows, axis=0)
        rotated = jnp.einsum(
            "sa,gsb->gab", own_coef, domain_rows, preferred_element_type=jnp.float32
        ).astype(jnp.bfloat16)[:, None]
    return (rotated, dressing[None])


def solution(mesh):
    return jax.shard_map(
        per_device,
        mesh=mesh,
        in_specs=(P("chol", "orb", None), P("orb"), P("orb", None, None), P(), P(), P()),
        out_specs=(P("chol", "orb", None, None), P("orb", None, None)),
        check_vma=False,
    )
```

```python
import math

import jax
import jax.numpy as jnp
from jax import lax
from jax.sharding import PartitionSpec as P


def split_bf16(x):
    hi = x.astype(jnp.bfloat16)
    rest = x - hi.astype(jnp.float32)
    mid = rest.astype(jnp.bfloat16)
    lo = (rest - mid.astype(jnp.float32)).astype(jnp.bfloat16)
    return jnp.stack([hi, mid, lo])


def join_bf16(parts):
    parts = parts.astype(jnp.float32)
    return (parts[0] + parts[1]) + parts[2]


def per_device(chol_vec, env_weight, lno_coef, domain, block_fill, lno_count):
    chol_local, orb_rows, orb_total = chol_vec.shape
    frag_total, slot_total = domain.shape
    group_count = block_fill.shape[1]
    group_width = slot_total // group_count
    lno_width = lno_coef.shape[2]
    chol_size = lax.axis_size("chol")
    orb_size = lax.axis_size("orb")
    my_index = lax.axis_index("orb")
    norm_factor = 1.0 / math.sqrt(chol_local * chol_size * orb_total)

    slot_index = jnp.arange(slot_total, dtype=jnp.int32)
    slot_ok = (slot_index % group_width)[None, :] < jnp.repeat(block_fill, group_width, axis=1)
    column_ok = jnp.arange(lno_width, dtype=jnp.int32)[None, :] < lno_count[:, None]
    keep_mask = (slot_ok[:, :, None] & column_ok[:, None, :]).astype(jnp.bfloat16)

    weight_rows = -(-3 * orb_rows // lno_width)
    pad_rows = -(-weight_rows // 8) * 8
    weight_parts = split_bf16(env_weight).reshape(-1)
    weight_parts = jnp.pad(weight_parts, (0, pad_rows * lno_width - weight_parts.shape[0]))
    payload = jnp.concatenate(
        [lno_coef, weight_parts.reshape(1, pad_rows, lno_width)], axis=1
    )
    gathered = lax.all_gather(payload, "orb", axis=0, tiled=True)
    all_coef = gathered[:, :slot_total]
    weight_all = join_bf16(
        gathered[:, slot_total:].reshape(orb_size, -1)[:, : 3 * orb_rows].reshape(orb_size, 3, orb_rows).transpose(1, 0, 2)
    )
    masked = all_coef * keep_mask

    with jax.named_scope("scatter_coef"):
        groups = domain.reshape(frag_total, group_count, group_width)
        group_block = groups[:, :, 0] // orb_rows
        block_ids = jnp.arange(orb_size, dtype=jnp.int32)
        sel = group_block[:, None, :] == block_ids[None, :, None]
        present = jnp.any(sel, axis=2)
        group_of_block = jnp.argmax(sel, axis=2).astype(jnp.int32)
        local = jnp.take_along_axis(groups, group_of_block[:, :, None], axis=1)
        local = local - block_ids[None, :, None] * orb_rows
        coef_groups = masked.reshape(frag_total, group_count, group_width, lno_width)
        coef_perm = jnp.take_along_axis(coef_groups, group_of_block[:, :, None, None], axis=1)
        row_ids = jnp.arange(orb_rows, dtype=jnp.int32)
        onehot = (
            (local[:, :, None, :] == row_ids[None, None, :, None]) & present[:, :, None, None]
        ).astype(jnp.bfloat16)
        w_full = jnp.einsum(
            "fbrs,fbsa->fbra", onehot, coef_perm, preferred_element_type=jnp.float32
        ).astype(jnp.bfloat16)

    with jax.named_scope("half"):
        half = jnp.einsum(
            "kc,fca->fka",
            chol_vec.reshape(chol_local * orb_rows, orb_total),
            w_full.reshape(frag_total, orb_size * orb_rows, lno_width),
            preferred_element_type=jnp.float32,
        ).astype(jnp.bfloat16)
        half = half.reshape(frag_total, chol_local, orb_rows, lno_width)

    received = lax.all_to_all(half, "orb", split_axis=0, concat_axis=0, tiled=True)

    with jax.named_scope("dressing"):
        weighted = (
            received.astype(jnp.float32) * weight_all.reshape(orb_size, 1, orb_rows, 1)
        ).astype(jnp.bfloat16)
        dressing_part = lax.dot_general(
            weighted.reshape(-1, lno_width),
            received.reshape(-1, lno_width),
            (((0,), (0,)), ((), ())),
            preferred_element_type=jnp.float32,
        )
        dressing = (lax.psum(dressing_part, "chol") * norm_factor).astype(jnp.bfloat16)

    with jax.named_scope("rotated"):
        own_w = lax.dynamic_index_in_dim(w_full, my_index, 0, keepdims=False)
        rotated = jnp.einsum(
            "ora,ogrb->gab", own_w, received, preferred_element_type=jnp.float32
        ).astype(jnp.bfloat16)[:, None]
    return (rotated, dressing[None])


def solution(mesh):
    return jax.shard_map(
        per_device,
        mesh=mesh,
        in_specs=(P("chol", "orb", None), P("orb"), P("orb", None, None), P(), P(), P()),
        out_specs=(P("chol", "orb", None, None), P("orb", None, None)),
        check_vma=False,
    )
```

```python
import math

import jax
import jax.numpy as jnp
from jax import lax
from jax.sharding import PartitionSpec as P


def split_bf16(x):
    hi = lax.reduce_precision(x, exponent_bits=8, mantissa_bits=7)
    rest = x - hi
    mid = lax.reduce_precision(rest, exponent_bits=8, mantissa_bits=7)
    lo = rest - mid
    return jnp.stack([hi, mid, lo]).astype(jnp.bfloat16)


def join_bf16(parts):
    parts = parts.astype(jnp.float32)
    return (parts[0] + parts[1]) + parts[2]


def per_device(chol_vec, env_weight, lno_coef, domain, block_fill, lno_count):
    chol_local, orb_rows, orb_total = chol_vec.shape
    frag_total, slot_total = domain.shape
    group_count = block_fill.shape[1]
    group_width = slot_total // group_count
    lno_width = lno_coef.shape[2]
    chol_size = lax.axis_size("chol")
    orb_size = lax.axis_size("orb")
    my_index = lax.axis_index("orb")
    norm_factor = 1.0 / math.sqrt(chol_local * chol_size * orb_total)
    chunks = lno_width // 128 if lno_width % 128 == 0 else 1
    width = lno_width // chunks

    slot_index = jnp.arange(slot_total, dtype=jnp.int32)
    slot_ok = (slot_index % group_width)[None, :] < jnp.repeat(block_fill, group_width, axis=1)
    column_ok = (jnp.arange(lno_width, dtype=jnp.int32)[None, :] < lno_count[:, None]).astype(jnp.float32)

    with jax.named_scope("placement"):
        groups = domain.reshape(frag_total, group_count, group_width)
        group_block = groups[:, :, 0] // orb_rows
        block_ids = jnp.arange(orb_size, dtype=jnp.int32)
        sel = group_block[:, None, :] == block_ids[None, :, None]
        present = jnp.any(sel, axis=2)
        group_of_block = jnp.argmax(sel, axis=2).astype(jnp.int32)
        local = jnp.take_along_axis(groups, group_of_block[:, :, None], axis=1)
        local = local - block_ids[None, :, None] * orb_rows
        slot_ok_perm = jnp.take_along_axis(
            slot_ok.reshape(frag_total, group_count, group_width), group_of_block[:, :, None], axis=1
        )
        row_ids = jnp.arange(orb_rows, dtype=jnp.int32)
        onehot = (
            (local[:, :, None, :] == row_ids[None, None, :, None])
            & (present[:, :, None] & slot_ok_perm)[:, :, None, :]
        ).astype(jnp.bfloat16)

    def place(coef, hot, group_pick, mask):
        picked = jnp.take_along_axis(coef, group_pick, axis=-3)
        placed = jnp.einsum("...brs,...bsa->...bra", hot, picked, preferred_element_type=jnp.float32)
        placed = placed * mask
        return placed.astype(jnp.bfloat16).reshape(placed.shape[:-3] + (-1, placed.shape[-1]))

    own_hot = lax.dynamic_index_in_dim(onehot, my_index, 0, keepdims=False)
    own_pick = lax.dynamic_index_in_dim(group_of_block, my_index, 0, keepdims=False)
    own_mask = lax.dynamic_index_in_dim(column_ok, my_index, 0, keepdims=False)
    own_w = place(
        lno_coef[0].reshape(group_count, group_width, lno_width),
        own_hot,
        own_pick[:, None, None],
        own_mask[None, None, :],
    )

    weight_rows = -(-3 * orb_rows // width)
    pad_rows = -(-weight_rows // 8) * 8
    weight_parts = split_bf16(env_weight).reshape(-1)
    weight_parts = jnp.pad(weight_parts, (0, pad_rows * width - weight_parts.shape[0]))

    chol2d = chol_vec.reshape(chol_local * orb_rows, orb_total)
    received = []
    weighted = []
    rot_parts = []
    blocks = {}
    weight_all = None
    for k in range(chunks):
        cols = slice(k * width, (k + 1) * width)
        payload = lno_coef[:, :, cols]
        if k == 0:
            payload = jnp.concatenate([payload, weight_parts.reshape(1, pad_rows, width)], axis=1)
        gathered = lax.all_gather(payload, "orb", axis=0, tiled=True)
        if k == 0:
            weight_all = join_bf16(
                gathered[:, slot_total:]
                .reshape(orb_size, -1)[:, : 3 * orb_rows]
                .reshape(orb_size, 3, orb_rows)
                .transpose(1, 0, 2)
            )
        with jax.named_scope("half"):
            w_k = place(
                gathered[:, :slot_total].reshape(frag_total, group_count, group_width, width),
                onehot,
                group_of_block[:, :, None, None],
                column_ok[:, None, None, cols],
            )
            half = jnp.einsum("kc,fca->fka", chol2d, w_k, preferred_element_type=jnp.float32)
            half = half.astype(jnp.bfloat16).reshape(frag_total, chol_local, orb_rows, width)
        recv = lax.all_to_all(half, "orb", split_axis=0, concat_axis=0, tiled=True)
        with jax.named_scope("dressing"):
            wtd = (recv.astype(jnp.float32) * weight_all.reshape(orb_size, 1, orb_rows, 1)).astype(jnp.bfloat16)
            received.append(recv.reshape(-1, width))
            weighted.append(wtd.reshape(-1, width))
            for j in range(k + 1):
                for a_i, b_i in {(k, j), (j, k)}:
                    blocks[(a_i, b_i)] = lax.dot_general(
                        weighted[a_i], received[b_i], (((0,), (0,)), ((), ())),
                        preferred_element_type=jnp.float32,
                    )
        with jax.named_scope("rotated"):
            rot_parts.append(
                jnp.einsum(
                    "ora,ogrb->gab", own_w.reshape(orb_size, orb_rows, lno_width), recv,
                    preferred_element_type=jnp.float32,
                ).astype(jnp.bfloat16)
            )

    with jax.named_scope("dressing"):
        dressing_part = jnp.concatenate(
            [jnp.concatenate([blocks[(i, j)] for j in range(chunks)], axis=1) for i in range(chunks)], axis=0
        )
        dressing = (lax.psum(dressing_part, "chol") * norm_factor).astype(jnp.bfloat16)
    rotated = jnp.concatenate(rot_parts, axis=2)[:, None]
    return (rotated, dressing[None])


def solution(mesh):
    return jax.shard_map(
        per_device,
        mesh=mesh,
        in_specs=(P("chol", "orb", None), P("orb"), P("orb", None, None), P(), P(), P()),
        out_specs=(P("chol", "orb", None, None), P("orb", None, None)),
        check_vma=False,
    )
```

```python
import math

import jax
import jax.numpy as jnp
from jax import lax
from jax.sharding import PartitionSpec as P


def split_bf16(x):
    hi = lax.reduce_precision(x, exponent_bits=8, mantissa_bits=7)
    rest = x - hi
    mid = lax.reduce_precision(rest, exponent_bits=8, mantissa_bits=7)
    lo = rest - mid
    return jnp.stack([hi, mid, lo]).astype(jnp.bfloat16)


def join_bf16(parts):
    parts = parts.astype(jnp.float32)
    return (parts[0] + parts[1]) + parts[2]


def swap(x, axis, size, step):
    return lax.ppermute(x, axis, [(i, i ^ step) for i in range(size)])


def per_device(chol_vec, env_weight, lno_coef, domain, block_fill, lno_count):
    chol_local, orb_rows, orb_total = chol_vec.shape
    frag_total, slot_total = domain.shape
    group_count = block_fill.shape[1]
    group_width = slot_total // group_count
    lno_width = lno_coef.shape[2]
    chol_size = lax.axis_size("chol")
    orb_size = lax.axis_size("orb")
    assert orb_size & (orb_size - 1) == 0 and chol_size & (chol_size - 1) == 0
    assert frag_total == orb_size
    my_index = lax.axis_index("orb")
    norm_factor = 1.0 / math.sqrt(chol_local * chol_size * orb_total)

    slot_index = jnp.arange(slot_total, dtype=jnp.int32)
    slot_ok = (slot_index % group_width)[None, :] < jnp.repeat(block_fill, group_width, axis=1)
    column_ok = (jnp.arange(lno_width, dtype=jnp.int32)[None, :] < lno_count[:, None]).astype(jnp.float32)

    with jax.named_scope("placement"):
        groups = domain.reshape(frag_total, group_count, group_width)
        group_block = groups[:, :, 0] // orb_rows
        block_ids = jnp.arange(orb_size, dtype=jnp.int32)
        sel = group_block[:, None, :] == block_ids[None, :, None]
        present = jnp.any(sel, axis=2)
        group_of_block = jnp.argmax(sel, axis=2).astype(jnp.int32)
        local = jnp.take_along_axis(groups, group_of_block[:, :, None], axis=1)
        local = local - block_ids[None, :, None] * orb_rows
        slot_ok_perm = jnp.take_along_axis(
            slot_ok.reshape(frag_total, group_count, group_width), group_of_block[:, :, None], axis=1
        )
        row_ids = jnp.arange(orb_rows, dtype=jnp.int32)
        onehot = (
            (local[:, :, None, :] == row_ids[None, None, :, None])
            & (present[:, :, None] & slot_ok_perm)[:, :, None, :]
        ).astype(jnp.bfloat16)

    def placed_coef(coef, frag):
        hot = lax.dynamic_index_in_dim(onehot, frag, 0, keepdims=False)
        pick = lax.dynamic_index_in_dim(group_of_block, frag, 0, keepdims=False)
        mask = lax.dynamic_index_in_dim(column_ok, frag, 0, keepdims=False)
        picked = jnp.take_along_axis(
            coef.reshape(group_count, group_width, lno_width), pick[:, None, None], axis=0
        )
        placed = jnp.einsum("brs,bsa->bra", hot, picked, preferred_element_type=jnp.float32)
        return (placed * mask).astype(jnp.bfloat16).reshape(orb_total, lno_width)

    chol2d = chol_vec.reshape(chol_local * orb_rows, orb_total)

    def half_of(coef, frag):
        with jax.named_scope("half"):
            return jnp.dot(
                chol2d, placed_coef(coef, frag), preferred_element_type=jnp.float32
            ).astype(jnp.bfloat16)

    own_coef = lno_coef[0]
    own_placed = placed_coef(own_coef, my_index)

    weight_rows = -(-3 * orb_rows // lno_width)
    pad_rows = -(-weight_rows // 8) * 8
    weight_parts = split_bf16(env_weight).reshape(-1)
    weight_parts = jnp.pad(weight_parts, (0, pad_rows * lno_width - weight_parts.shape[0]))
    payload = jnp.concatenate([own_coef, weight_parts.reshape(pad_rows, lno_width)], axis=0)

    def absorb(acc, rows, weights, block):
        dress, rot = acc
        with jax.named_scope("dressing"):
            wtd = (
                rows.reshape(chol_local, orb_rows, lno_width).astype(jnp.float32)
                * weights[None, :, None]
            ).astype(jnp.bfloat16)
            dress = dress + lax.dot_general(
                wtd.reshape(-1, lno_width), rows, (((0,), (0,)), ((), ())),
                preferred_element_type=jnp.float32,
            )
        with jax.named_scope("rotated"):
            coef_rows = lax.dynamic_slice_in_dim(own_placed, block * orb_rows, orb_rows)
            rot = rot + jnp.einsum(
                "ra,grb->gab", coef_rows, rows.reshape(chol_local, orb_rows, lno_width),
                preferred_element_type=jnp.float32,
            )
        return dress, rot

    acc = (
        jnp.zeros((lno_width, lno_width), jnp.float32),
        jnp.zeros((chol_local, lno_width, lno_width), jnp.float32),
    )
    acc = absorb(acc, half_of(own_coef, my_index), env_weight, my_index)
    steps = sorted(range(1, orb_size), key=lambda s: (bin(s).count("1"), s))
    for step in steps:
        partner = my_index ^ step
        got = swap(payload, "orb", orb_size, step)
        half = half_of(got[:slot_total], partner)
        back = swap(half, "orb", orb_size, step)
        weights = join_bf16(got[slot_total:].reshape(-1)[: 3 * orb_rows].reshape(3, orb_rows))
        acc = absorb(acc, back, weights, partner)

    dress, rot = acc
    with jax.named_scope("chol_sum"):
        step = 1
        while step < chol_size:
            dress = dress + swap(dress, "chol", chol_size, step)
            step *= 2
    dressing = (dress * norm_factor).astype(jnp.bfloat16)
    rotated = rot.astype(jnp.bfloat16)[:, None]
    return (rotated, dressing[None])


def solution(mesh):
    return jax.shard_map(
        per_device,
        mesh=mesh,
        in_specs=(P("chol", "orb", None), P("orb"), P("orb", None, None), P(), P(), P()),
        out_specs=(P("chol", "orb", None, None), P("orb", None, None)),
        check_vma=False,
    )
```

```python
import math

import jax
import jax.numpy as jnp
from jax import lax
from jax.sharding import PartitionSpec as P


def split_bf16(x):
    hi = lax.reduce_precision(x, exponent_bits=8, mantissa_bits=7)
    rest = x - hi
    mid = lax.reduce_precision(rest, exponent_bits=8, mantissa_bits=7)
    lo = rest - mid
    return jnp.stack([hi, mid, lo]).astype(jnp.bfloat16)


def join_bf16(parts):
    parts = parts.astype(jnp.float32)
    return (parts[0] + parts[1]) + parts[2]


def per_device(chol_vec, env_weight, lno_coef, domain, block_fill, lno_count):
    chol_local, orb_rows, orb_total = chol_vec.shape
    frag_total, slot_total = domain.shape
    group_count = block_fill.shape[1]
    group_width = slot_total // group_count
    lno_width = lno_coef.shape[2]
    chol_size = lax.axis_size("chol")
    orb_size = lax.axis_size("orb")
    my_index = lax.axis_index("orb")
    norm_factor = 1.0 / math.sqrt(chol_local * chol_size * orb_total)
    chunks = lno_width // 128 if lno_width % 128 == 0 else 1
    width = lno_width // chunks

    slot_index = jnp.arange(slot_total, dtype=jnp.int32)
    slot_ok = (slot_index % group_width)[None, :] < jnp.repeat(block_fill, group_width, axis=1)
    column_ok = jnp.arange(lno_width, dtype=jnp.int32)[None, :] < lno_count[:, None]

    weight_rows = -(-3 * orb_rows // lno_width)
    pad_rows = -(-weight_rows // 8) * 8
    weight_parts = split_bf16(env_weight).reshape(-1)
    weight_parts = jnp.pad(weight_parts, (0, pad_rows * lno_width - weight_parts.shape[0]))
    payload = jnp.concatenate([lno_coef, weight_parts.reshape(1, pad_rows, lno_width)], axis=1)
    gathered = lax.all_gather(payload, "orb", axis=0, tiled=True)

    with jax.named_scope("pick_columns"):
        chol_t = chol_vec.reshape(chol_local * orb_rows, orb_total).T
        picked = jnp.take(chol_t, domain, axis=0)
        picked = jnp.where(slot_ok[:, :, None], picked, jnp.zeros_like(picked))

    with jax.named_scope("own_placement"):
        own_groups = lax.dynamic_index_in_dim(domain, my_index, 0, keepdims=False)
        own_groups = own_groups.reshape(group_count, group_width)
        own_fill = lax.dynamic_index_in_dim(slot_ok, my_index, 0, keepdims=False)
        own_fill = own_fill.reshape(group_count, group_width)
        own_cols = lax.dynamic_index_in_dim(column_ok, my_index, 0, keepdims=False)
        block_ids = jnp.arange(orb_size, dtype=jnp.int32)
        sel = (own_groups[:, 0] // orb_rows)[None, :] == block_ids[:, None]
        present = jnp.any(sel, axis=1)
        group_of_block = jnp.argmax(sel, axis=1).astype(jnp.int32)
        local = jnp.take(own_groups, group_of_block, axis=0) - block_ids[:, None] * orb_rows
        fill = jnp.take(own_fill, group_of_block, axis=0) & present[:, None]
        row_ids = jnp.arange(orb_rows, dtype=jnp.int32)
        onehot = ((local[:, None, :] == row_ids[None, :, None]) & fill[:, None, :]).astype(jnp.bfloat16)
        own_coef = jnp.take(lno_coef[0].reshape(group_count, group_width, lno_width), group_of_block, axis=0)
        own_w = jnp.einsum("brs,bsa->bra", onehot, own_coef, preferred_element_type=jnp.float32)
        own_w = jnp.where(own_cols[None, None, :], own_w, 0.0).astype(jnp.bfloat16)

    all_coef = gathered[:, :slot_total]
    weight_all = join_bf16(
        gathered[:, slot_total:]
        .reshape(orb_size, -1)[:, : 3 * orb_rows]
        .reshape(orb_size, 3, orb_rows)
        .transpose(1, 0, 2)
    )

    received = []
    weighted = []
    rot_parts = []
    blocks = {}
    for k in range(chunks):
        cols = slice(k * width, (k + 1) * width)
        with jax.named_scope("half"):
            half = jnp.einsum(
                "fsk,fsa->fka", picked, all_coef[:, :, cols], preferred_element_type=jnp.float32
            )
            half = jnp.where(column_ok[:, None, cols], half, 0.0).astype(jnp.bfloat16)
            half = half.reshape(frag_total, chol_local, orb_rows, width)
        recv = lax.all_to_all(half, "orb", split_axis=0, concat_axis=0, tiled=True)
        with jax.named_scope("dressing"):
            wtd = (recv.astype(jnp.float32) * weight_all.reshape(orb_size, 1, orb_rows, 1)).astype(jnp.bfloat16)
            received.append(recv.reshape(-1, width))
            weighted.append(wtd.reshape(-1, width))
            pairs = [(k, k)] + [p for j in range(k) for p in ((k, j), (j, k))]
            for a_i, b_i in pairs:
                blocks[(a_i, b_i)] = lax.dot_general(
                    weighted[a_i], received[b_i], (((0,), (0,)), ((), ())),
                    preferred_element_type=jnp.float32,
                )
        with jax.named_scope("rotated"):
            rot_parts.append(
                jnp.einsum(
                    "ora,ogrb->gab", own_w, recv, preferred_element_type=jnp.float32
                ).astype(jnp.bfloat16)
            )

    with jax.named_scope("dressing"):
        dressing_part = jnp.concatenate(
            [jnp.concatenate([blocks[(i, j)] for j in range(chunks)], axis=1) for i in range(chunks)], axis=0
        )
        dressing = (lax.psum(dressing_part, "chol") * norm_factor).astype(jnp.bfloat16)
    rotated = jnp.concatenate(rot_parts, axis=2)[:, None]
    return (rotated, dressing[None])


def solution(mesh):
    return jax.shard_map(
        per_device,
        mesh=mesh,
        in_specs=(P("chol", "orb", None), P("orb"), P("orb", None, None), P(), P(), P()),
        out_specs=(P("chol", "orb", None, None), P("orb", None, None)),
        check_vma=False,
    )
```

```python
import math

import jax
import jax.numpy as jnp
from jax import lax
from jax.sharding import PartitionSpec as P


def split_bf16(x):
    hi = lax.reduce_precision(x, exponent_bits=8, mantissa_bits=7)
    rest = x - hi
    mid = lax.reduce_precision(rest, exponent_bits=8, mantissa_bits=7)
    lo = rest - mid
    return jnp.stack([hi, mid, lo]).astype(jnp.bfloat16)


def join_bf16(parts):
    parts = parts.astype(jnp.float32)
    return (parts[0] + parts[1]) + parts[2]


def per_device(chol_vec, env_weight, lno_coef, domain, block_fill, lno_count):
    chol_local, orb_rows, orb_total = chol_vec.shape
    frag_total, slot_total = domain.shape
    group_count = block_fill.shape[1]
    group_width = slot_total // group_count
    lno_width = lno_coef.shape[2]
    chol_size = lax.axis_size("chol")
    orb_size = lax.axis_size("orb")
    my_index = lax.axis_index("orb")
    norm_factor = 1.0 / math.sqrt(chol_local * chol_size * orb_total)

    slot_index = jnp.arange(slot_total, dtype=jnp.int32)
    slot_ok = (slot_index % group_width)[None, :] < jnp.repeat(block_fill, group_width, axis=1)
    column_ok = jnp.arange(lno_width, dtype=jnp.int32)[None, :] < lno_count[:, None]

    weight_rows = -(-3 * orb_rows // lno_width)
    pad_rows = -(-weight_rows // 8) * 8
    weight_parts = split_bf16(env_weight).reshape(-1)
    weight_parts = jnp.pad(weight_parts, (0, pad_rows * lno_width - weight_parts.shape[0]))
    payload = jnp.concatenate([lno_coef, weight_parts.reshape(1, pad_rows, lno_width)], axis=1)
    gathered = lax.all_gather(payload, "orb", axis=0, tiled=True)

    with jax.named_scope("pick_columns"):
        chol_t = chol_vec.reshape(chol_local * orb_rows, orb_total).T
        picked = jnp.take(chol_t, domain, axis=0)
        picked = jnp.where(slot_ok[:, :, None], picked, jnp.zeros_like(picked))

    with jax.named_scope("own_placement"):
        own_groups = lax.dynamic_index_in_dim(domain, my_index, 0, keepdims=False)
        own_groups = own_groups.reshape(group_count, group_width)
        own_fill = lax.dynamic_index_in_dim(slot_ok, my_index, 0, keepdims=False)
        own_fill = own_fill.reshape(group_count, group_width)
        own_cols = lax.dynamic_index_in_dim(column_ok, my_index, 0, keepdims=False)
        block_ids = jnp.arange(orb_size, dtype=jnp.int32)
        sel = (own_groups[:, 0] // orb_rows)[None, :] == block_ids[:, None]
        present = jnp.any(sel, axis=1)
        group_of_block = jnp.argmax(sel, axis=1).astype(jnp.int32)
        local = jnp.take(own_groups, group_of_block, axis=0) - block_ids[:, None] * orb_rows
        fill = jnp.take(own_fill, group_of_block, axis=0) & present[:, None]
        row_ids = jnp.arange(orb_rows, dtype=jnp.int32)
        onehot = ((local[:, None, :] == row_ids[None, :, None]) & fill[:, None, :]).astype(jnp.bfloat16)
        own_coef = jnp.take(lno_coef[0].reshape(group_count, group_width, lno_width), group_of_block, axis=0)
        own_w = jnp.einsum("brs,bsa->bra", onehot, own_coef, preferred_element_type=jnp.float32)
        own_w = jnp.where(own_cols[None, None, :], own_w, 0.0).astype(jnp.bfloat16)

    all_coef = gathered[:, :slot_total]
    weight_all = join_bf16(
        gathered[:, slot_total:]
        .reshape(orb_size, -1)[:, : 3 * orb_rows]
        .reshape(orb_size, 3, orb_rows)
        .transpose(1, 0, 2)
    )

    with jax.named_scope("half"):
        half = jnp.einsum("fsk,fsa->fka", picked, all_coef, preferred_element_type=jnp.float32)
        half = jnp.where(column_ok[:, None, :], half, 0.0).astype(jnp.bfloat16)
        half = half.reshape(frag_total, chol_local, orb_rows, lno_width)

    received = lax.all_to_all(half, "orb", split_axis=0, concat_axis=0, tiled=True)

    with jax.named_scope("dressing"):
        weighted = (
            received.astype(jnp.float32) * weight_all.reshape(orb_size, 1, orb_rows, 1)
        ).astype(jnp.bfloat16)
        dressing_part = lax.dot_general(
            weighted.reshape(-1, lno_width),
            received.reshape(-1, lno_width),
            (((0,), (0,)), ((), ())),
            preferred_element_type=jnp.float32,
        )
        dressing = (lax.psum(dressing_part, "chol") * norm_factor).astype(jnp.bfloat16)

    with jax.named_scope("rotated"):
        rotated = jnp.einsum(
            "ora,ogrb->gab", own_w, received, preferred_element_type=jnp.float32
        ).astype(jnp.bfloat16)[:, None]
    return (rotated, dressing[None])


def solution(mesh):
    return jax.shard_map(
        per_device,
        mesh=mesh,
        in_specs=(P("chol", "orb", None), P("orb"), P("orb", None, None), P(), P(), P()),
        out_specs=(P("chol", "orb", None, None), P("orb", None, None)),
        check_vma=False,
    )
```

```python
import math

import jax
import jax.numpy as jnp
from jax import lax
from jax.sharding import PartitionSpec as P


def split_bf16(x):
    hi = lax.reduce_precision(x, exponent_bits=8, mantissa_bits=7)
    rest = x - hi
    mid = lax.reduce_precision(rest, exponent_bits=8, mantissa_bits=7)
    lo = rest - mid
    return jnp.stack([hi, mid, lo]).astype(jnp.bfloat16)


def join_bf16(parts):
    parts = parts.astype(jnp.float32)
    return (parts[0] + parts[1]) + parts[2]


def per_device(chol_vec, env_weight, lno_coef, domain, block_fill, lno_count):
    chol_local, orb_rows, orb_total = chol_vec.shape
    frag_total, slot_total = domain.shape
    group_count = block_fill.shape[1]
    group_width = slot_total // group_count
    lno_width = lno_coef.shape[2]
    chol_size = lax.axis_size("chol")
    orb_size = lax.axis_size("orb")
    my_index = lax.axis_index("orb")
    norm_factor = 1.0 / math.sqrt(chol_local * chol_size * orb_total)

    slot_index = jnp.arange(slot_total, dtype=jnp.int32)
    slot_ok = (slot_index % group_width)[None, :] < jnp.repeat(block_fill, group_width, axis=1)
    column_ok = jnp.arange(lno_width, dtype=jnp.int32)[None, :] < lno_count[:, None]

    weight_rows = -(-3 * orb_rows // lno_width)
    pad_rows = -(-weight_rows // 8) * 8
    weight_parts = split_bf16(env_weight).reshape(-1)
    weight_parts = jnp.pad(weight_parts, (0, pad_rows * lno_width - weight_parts.shape[0]))
    payload = jnp.concatenate([lno_coef, weight_parts.reshape(1, pad_rows, lno_width)], axis=1)
    gathered = lax.all_gather(payload, "orb", axis=0, tiled=True)

    with jax.named_scope("pick_columns"):
        chol_t = chol_vec.reshape(chol_local * orb_rows, orb_total).T
        picked = jnp.take(chol_t, domain, axis=0)
        picked = jnp.where(slot_ok[:, :, None], picked, jnp.zeros_like(picked))

    with jax.named_scope("own_placement"):
        own_groups = lax.dynamic_index_in_dim(domain, my_index, 0, keepdims=False)
        own_groups = own_groups.reshape(group_count, group_width)
        own_fill = lax.dynamic_index_in_dim(slot_ok, my_index, 0, keepdims=False)
        own_fill = own_fill.reshape(group_count, group_width)
        own_cols = lax.dynamic_index_in_dim(column_ok, my_index, 0, keepdims=False)
        block_ids = jnp.arange(orb_size, dtype=jnp.int32)
        sel = (own_groups[:, 0] // orb_rows)[None, :] == block_ids[:, None]
        present = jnp.any(sel, axis=1)
        group_of_block = jnp.argmax(sel, axis=1).astype(jnp.int32)
        local = jnp.take(own_groups, group_of_block, axis=0) - block_ids[:, None] * orb_rows
        fill = jnp.take(own_fill, group_of_block, axis=0) & present[:, None]
        row_ids = jnp.arange(orb_rows, dtype=jnp.int32)
        onehot = ((local[:, None, :] == row_ids[None, :, None]) & fill[:, None, :]).astype(jnp.bfloat16)
        own_coef = jnp.take(lno_coef[0].reshape(group_count, group_width, lno_width), group_of_block, axis=0)
        own_w = jnp.einsum("brs,bsa->bra", onehot, own_coef, preferred_element_type=jnp.float32)
        own_w = jnp.where(own_cols[None, None, :], own_w, 0.0).astype(jnp.bfloat16)

    all_coef = gathered[:, :slot_total]
    weight_all = join_bf16(
        gathered[:, slot_total:]
        .reshape(orb_size, -1)[:, : 3 * orb_rows]
        .reshape(orb_size, 3, orb_rows)
        .transpose(1, 0, 2)
    )

    with jax.named_scope("half"):
        half = jnp.einsum("fsk,fsa->fka", picked, all_coef, preferred_element_type=jnp.float32)
        half = jnp.where(column_ok[:, None, :], half, 0.0).astype(jnp.bfloat16)
        half = half.reshape(frag_total, chol_local, orb_rows, lno_width)

    received = lax.all_to_all(half, "orb", split_axis=0, concat_axis=0, tiled=True)

    with jax.named_scope("dressing"):
        weighted = (
            received.astype(jnp.float32) * weight_all.reshape(orb_size, 1, orb_rows, 1)
        ).astype(jnp.bfloat16)
        dressing_part = lax.dot_general(
            weighted.reshape(-1, lno_width),
            received.reshape(-1, lno_width),
            (((0,), (0,)), ((), ())),
            preferred_element_type=jnp.float32,
        )
    with jax.named_scope("chol_sum"):
        hi = lax.reduce_precision(dressing_part, exponent_bits=8, mantissa_bits=7)
        parts = jnp.stack([hi, dressing_part - hi]).astype(jnp.bfloat16)
        every = lax.all_gather(parts, "chol", axis=0, tiled=False).astype(jnp.float32)
        terms = every[:, 0] + every[:, 1]
        total = terms[0]
        for c in range(1, chol_size):
            total = total + terms[c]
        dressing = (total * norm_factor).astype(jnp.bfloat16)

    with jax.named_scope("rotated"):
        rotated = jnp.einsum(
            "ora,ogrb->gab", own_w, received, preferred_element_type=jnp.float32
        ).astype(jnp.bfloat16)[:, None]
    return (rotated, dressing[None])


def solution(mesh):
    return jax.shard_map(
        per_device,
        mesh=mesh,
        in_specs=(P("chol", "orb", None), P("orb"), P("orb", None, None), P(), P(), P()),
        out_specs=(P("chol", "orb", None, None), P("orb", None, None)),
        check_vma=False,
    )
```

```python
import math

import jax
import jax.numpy as jnp
from jax import lax
from jax.sharding import PartitionSpec as P


def split_bf16(x):
    hi = lax.reduce_precision(x, exponent_bits=8, mantissa_bits=7)
    rest = x - hi
    mid = lax.reduce_precision(rest, exponent_bits=8, mantissa_bits=7)
    lo = rest - mid
    return jnp.stack([hi, mid, lo]).astype(jnp.bfloat16)


def join_bf16(parts):
    parts = parts.astype(jnp.float32)
    return (parts[0] + parts[1]) + parts[2]


def per_device(chol_vec, env_weight, lno_coef, domain, block_fill, lno_count):
    chol_local, orb_rows, orb_total = chol_vec.shape
    frag_total, slot_total = domain.shape
    group_count = block_fill.shape[1]
    group_width = slot_total // group_count
    lno_width = lno_coef.shape[2]
    chol_size = lax.axis_size("chol")
    orb_size = lax.axis_size("orb")
    my_index = lax.axis_index("orb")
    norm_factor = 1.0 / math.sqrt(chol_local * chol_size * orb_total)

    slot_index = jnp.arange(slot_total, dtype=jnp.int32)
    slot_ok = (slot_index % group_width)[None, :] < jnp.repeat(block_fill, group_width, axis=1)
    column_ok = jnp.arange(lno_width, dtype=jnp.int32)[None, :] < lno_count[:, None]

    with jax.named_scope("placement"):
        groups = domain.reshape(frag_total, group_count, group_width)
        group_block = groups[:, :, 0] // orb_rows
        block_ids = jnp.arange(orb_size, dtype=jnp.int32)
        sel = group_block[:, None, :] == block_ids[None, :, None]
        present = jnp.any(sel, axis=2)
        group_of_block = jnp.argmax(sel, axis=2).astype(jnp.int32)
        local = jnp.take_along_axis(groups, group_of_block[:, :, None], axis=1)
        local = local - block_ids[None, :, None] * orb_rows
        fill = jnp.take_along_axis(
            slot_ok.reshape(frag_total, group_count, group_width), group_of_block[:, :, None], axis=1
        ) & present[:, :, None]
        row_ids = jnp.arange(orb_rows, dtype=jnp.int32)
        onehot = ((local[:, :, None, :] == row_ids[None, None, :, None]) & fill[:, :, None, :]).astype(jnp.bfloat16)

    own_pick = lax.dynamic_index_in_dim(group_of_block, my_index, 0, keepdims=False)
    own_perm = jnp.take(lno_coef[0].reshape(group_count, group_width, lno_width), own_pick, axis=0)
    weight_rows = -(-3 * orb_rows // lno_width)
    pad_rows = -(-weight_rows // 8) * 8
    weight_parts = split_bf16(env_weight).reshape(-1)
    weight_parts = jnp.pad(weight_parts, (0, pad_rows * lno_width - weight_parts.shape[0]))
    block_slots = orb_size * group_width
    payload = jnp.concatenate(
        [own_perm.reshape(1, block_slots, lno_width), weight_parts.reshape(1, pad_rows, lno_width)], axis=1
    )
    gathered = lax.all_gather(payload, "orb", axis=0, tiled=True)

    with jax.named_scope("pick_columns"):
        chol_blocks = chol_vec.reshape(chol_local * orb_rows, orb_size, orb_rows)
        picked = jnp.einsum(
            "kor,forc->fkoc", chol_blocks, onehot, preferred_element_type=jnp.float32
        ).astype(jnp.bfloat16).reshape(frag_total, chol_local * orb_rows, block_slots)

    with jax.named_scope("own_placement"):
        own_hot = lax.dynamic_index_in_dim(onehot, my_index, 0, keepdims=False)
        own_cols = lax.dynamic_index_in_dim(column_ok, my_index, 0, keepdims=False)
        own_w = jnp.einsum("orc,oca->ora", own_hot, own_perm, preferred_element_type=jnp.float32)
        own_w = jnp.where(own_cols[None, None, :], own_w, 0.0).astype(jnp.bfloat16)

    all_coef = gathered[:, :block_slots]
    weight_all = join_bf16(
        gathered[:, block_slots:]
        .reshape(orb_size, -1)[:, : 3 * orb_rows]
        .reshape(orb_size, 3, orb_rows)
        .transpose(1, 0, 2)
    )

    with jax.named_scope("half"):
        half = jnp.einsum("fks,fsa->fka", picked, all_coef, preferred_element_type=jnp.float32)
        half = jnp.where(column_ok[:, None, :], half, 0.0).astype(jnp.bfloat16)
        half = half.reshape(frag_total, chol_local, orb_rows, lno_width)

    received = lax.all_to_all(half, "orb", split_axis=0, concat_axis=0, tiled=True)

    with jax.named_scope("dressing"):
        weighted = (
            received.astype(jnp.float32) * weight_all.reshape(orb_size, 1, orb_rows, 1)
        ).astype(jnp.bfloat16)
        dressing_part = lax.dot_general(
            weighted.reshape(-1, lno_width),
            received.reshape(-1, lno_width),
            (((0,), (0,)), ((), ())),
            preferred_element_type=jnp.float32,
        )
        dressing = (lax.psum(dressing_part, "chol") * norm_factor).astype(jnp.bfloat16)

    with jax.named_scope("rotated"):
        rotated = jnp.einsum(
            "ora,ogrb->gab", own_w, received, preferred_element_type=jnp.float32
        ).astype(jnp.bfloat16)[:, None]
    return (rotated, dressing[None])


def solution(mesh):
    return jax.shard_map(
        per_device,
        mesh=mesh,
        in_specs=(P("chol", "orb", None), P("orb"), P("orb", None, None), P(), P(), P()),
        out_specs=(P("chol", "orb", None, None), P("orb", None, None)),
        check_vma=False,
    )
```

```python
import math

import jax
import jax.numpy as jnp
from jax import lax
from jax.sharding import PartitionSpec as P


def split_bf16(x):
    hi = lax.reduce_precision(x, exponent_bits=8, mantissa_bits=7)
    rest = x - hi
    mid = lax.reduce_precision(rest, exponent_bits=8, mantissa_bits=7)
    lo = rest - mid
    return jnp.stack([hi, mid, lo]).astype(jnp.bfloat16)


def join_bf16(parts):
    parts = parts.astype(jnp.float32)
    return (parts[0] + parts[1]) + parts[2]


def per_device(chol_vec, env_weight, lno_coef, domain, block_fill, lno_count):
    chol_local, orb_rows, orb_total = chol_vec.shape
    frag_total, slot_total = domain.shape
    group_count = block_fill.shape[1]
    group_width = slot_total // group_count
    lno_width = lno_coef.shape[2]
    chol_size = lax.axis_size("chol")
    orb_size = lax.axis_size("orb")
    my_index = lax.axis_index("orb")
    norm_factor = 1.0 / math.sqrt(chol_local * chol_size * orb_total)

    slot_index = jnp.arange(slot_total, dtype=jnp.int32)
    slot_ok = (slot_index % group_width)[None, :] < jnp.repeat(block_fill, group_width, axis=1)
    column_ok = jnp.arange(lno_width, dtype=jnp.int32)[None, :] < lno_count[:, None]

    with jax.named_scope("placement"):
        groups = domain.reshape(frag_total, group_count, group_width)
        group_block = groups[:, :, 0] // orb_rows
        block_ids = jnp.arange(orb_size, dtype=jnp.int32)
        sel = group_block[:, None, :] == block_ids[None, :, None]
        present = jnp.any(sel, axis=2)
        group_of_block = jnp.argmax(sel, axis=2).astype(jnp.int32)
        local = jnp.take_along_axis(groups, group_of_block[:, :, None], axis=1)
        local = local - block_ids[None, :, None] * orb_rows
        fill = jnp.take_along_axis(
            slot_ok.reshape(frag_total, group_count, group_width), group_of_block[:, :, None], axis=1
        ) & present[:, :, None]
        row_ids = jnp.arange(orb_rows, dtype=jnp.int32)
        onehot = ((local[:, :, None, :] == row_ids[None, None, :, None]) & fill[:, :, None, :]).astype(jnp.bfloat16)

    own_pick = lax.dynamic_index_in_dim(group_of_block, my_index, 0, keepdims=False)
    own_slots = lax.dynamic_index_in_dim(slot_ok, my_index, 0, keepdims=False)
    own_cols = lax.dynamic_index_in_dim(column_ok, my_index, 0, keepdims=False)
    own_masked = jnp.where(own_slots[:, None] & own_cols[None, :], lno_coef[0], jnp.zeros_like(lno_coef[0]))
    own_perm = jnp.take(own_masked.reshape(group_count, group_width, lno_width), own_pick, axis=0)
    weight_rows = -(-3 * orb_rows // lno_width)
    pad_rows = -(-weight_rows // 8) * 8
    weight_parts = split_bf16(env_weight).reshape(-1)
    weight_parts = jnp.pad(weight_parts, (0, pad_rows * lno_width - weight_parts.shape[0]))
    block_slots = orb_size * group_width
    payload = jnp.concatenate(
        [own_perm.reshape(1, block_slots, lno_width), weight_parts.reshape(1, pad_rows, lno_width)], axis=1
    )
    gathered = lax.all_gather(payload, "orb", axis=0, tiled=True)

    with jax.named_scope("pick_columns"):
        chol_blocks = chol_vec.reshape(chol_local * orb_rows, orb_size, orb_rows)
        picked = jnp.einsum(
            "kor,forc->fkoc", chol_blocks, onehot, preferred_element_type=jnp.float32
        ).astype(jnp.bfloat16).reshape(frag_total, chol_local * orb_rows, block_slots)

    with jax.named_scope("own_placement"):
        own_hot = lax.dynamic_index_in_dim(onehot, my_index, 0, keepdims=False)
        own_w = jnp.einsum(
            "orc,oca->ora", own_hot, own_perm, preferred_element_type=jnp.float32
        ).astype(jnp.bfloat16)

    all_coef = gathered[:, :block_slots]
    weight_all = join_bf16(
        gathered[:, block_slots:]
        .reshape(orb_size, -1)[:, : 3 * orb_rows]
        .reshape(orb_size, 3, orb_rows)
        .transpose(1, 0, 2)
    )

    with jax.named_scope("half"):
        half = jnp.einsum("fks,fsa->fka", picked, all_coef, preferred_element_type=jnp.float32)
        half = half.astype(jnp.bfloat16)
        half = half.reshape(frag_total, chol_local, orb_rows, lno_width)

    received = lax.all_to_all(half, "orb", split_axis=0, concat_axis=0, tiled=True)

    with jax.named_scope("dressing"):
        weighted = (
            received.astype(jnp.float32) * weight_all.reshape(orb_size, 1, orb_rows, 1)
        ).astype(jnp.bfloat16)
        dressing_part = lax.dot_general(
            weighted.reshape(-1, lno_width),
            received.reshape(-1, lno_width),
            (((0,), (0,)), ((), ())),
            preferred_element_type=jnp.float32,
        )
        dressing = (lax.psum(dressing_part, "chol") * norm_factor).astype(jnp.bfloat16)

    with jax.named_scope("rotated"):
        rotated = jnp.einsum(
            "ora,ogrb->gab", own_w, received, preferred_element_type=jnp.float32
        ).astype(jnp.bfloat16)[:, None]
    return (rotated, dressing[None])


def solution(mesh):
    return jax.shard_map(
        per_device,
        mesh=mesh,
        in_specs=(P("chol", "orb", None), P("orb"), P("orb", None, None), P(), P(), P()),
        out_specs=(P("chol", "orb", None, None), P("orb", None, None)),
        check_vma=False,
    )
```

```python
import math

import jax
import jax.numpy as jnp
from jax import lax
from jax.sharding import PartitionSpec as P


def split_bf16(x):
    hi = lax.reduce_precision(x, exponent_bits=8, mantissa_bits=7)
    rest = x - hi
    mid = lax.reduce_precision(rest, exponent_bits=8, mantissa_bits=7)
    lo = rest - mid
    return jnp.stack([hi, mid, lo]).astype(jnp.bfloat16)


def join_bf16(parts):
    parts = parts.astype(jnp.float32)
    return (parts[0] + parts[1]) + parts[2]


def per_device(chol_vec, env_weight, lno_coef, domain, block_fill, lno_count):
    chol_local, orb_rows, orb_total = chol_vec.shape
    frag_total, slot_total = domain.shape
    group_count = block_fill.shape[1]
    group_width = slot_total // group_count
    lno_width = lno_coef.shape[2]
    chol_size = lax.axis_size("chol")
    orb_size = lax.axis_size("orb")
    my_index = lax.axis_index("orb")
    norm_factor = 1.0 / math.sqrt(chol_local * chol_size * orb_total)

    slot_index = jnp.arange(slot_total, dtype=jnp.int32)
    slot_ok = (slot_index % group_width)[None, :] < jnp.repeat(block_fill, group_width, axis=1)
    column_ok = jnp.arange(lno_width, dtype=jnp.int32)[None, :] < lno_count[:, None]

    with jax.named_scope("placement"):
        groups = domain.reshape(frag_total, group_count, group_width)
        group_block = groups[:, :, 0] // orb_rows
        block_ids = jnp.arange(orb_size, dtype=jnp.int32)
        sel = group_block[:, None, :] == block_ids[None, :, None]
        present = jnp.any(sel, axis=2)
        group_of_block = jnp.argmax(sel, axis=2).astype(jnp.int32)
        local = jnp.take_along_axis(groups, group_of_block[:, :, None], axis=1)
        local = local - block_ids[None, :, None] * orb_rows
        fill = jnp.take_along_axis(
            slot_ok.reshape(frag_total, group_count, group_width), group_of_block[:, :, None], axis=1
        ) & present[:, :, None]
        row_ids = jnp.arange(orb_rows, dtype=jnp.int32)
        onehot = ((local[:, :, None, :] == row_ids[None, None, :, None]) & fill[:, :, None, :]).astype(jnp.bfloat16)

    own_pick = lax.dynamic_index_in_dim(group_of_block, my_index, 0, keepdims=False)
    own_perm = jnp.take(lno_coef[0].reshape(group_count, group_width, lno_width), own_pick, axis=0)
    weight_rows = -(-3 * orb_rows // lno_width)
    pad_rows = -(-weight_rows // 8) * 8
    weight_parts = split_bf16(env_weight).reshape(-1)
    weight_parts = jnp.pad(weight_parts, (0, pad_rows * lno_width - weight_parts.shape[0]))
    payload = jnp.concatenate([lno_coef, weight_parts.reshape(1, pad_rows, lno_width)], axis=1)
    gathered = lax.all_gather(payload, "orb", axis=0, tiled=True)

    with jax.named_scope("pick_columns"):
        group_rows = groups - group_block[:, :, None] * orb_rows
        group_hot = (
            (group_rows[:, :, None, :] == row_ids[None, None, :, None])
            & slot_ok.reshape(frag_total, group_count, group_width)[:, :, None, :]
        ).astype(jnp.bfloat16)
        chol_blocks = chol_vec.reshape(chol_local * orb_rows, orb_size, orb_rows).transpose(1, 0, 2)
        chol_groups = jnp.take(chol_blocks, group_block, axis=0)
        picked = jnp.einsum(
            "fjkr,fjrc->fkjc", chol_groups, group_hot, preferred_element_type=jnp.float32
        ).astype(jnp.bfloat16).reshape(frag_total, chol_local * orb_rows, slot_total)

    with jax.named_scope("own_placement"):
        own_hot = lax.dynamic_index_in_dim(onehot, my_index, 0, keepdims=False)
        own_cols = lax.dynamic_index_in_dim(column_ok, my_index, 0, keepdims=False)
        own_w = jnp.einsum("orc,oca->ora", own_hot, own_perm, preferred_element_type=jnp.float32)
        own_w = jnp.where(own_cols[None, None, :], own_w, 0.0).astype(jnp.bfloat16)

    all_coef = gathered[:, :slot_total]
    weight_all = join_bf16(
        gathered[:, slot_total:]
        .reshape(orb_size, -1)[:, : 3 * orb_rows]
        .reshape(orb_size, 3, orb_rows)
        .transpose(1, 0, 2)
    )

    with jax.named_scope("half"):
        half = jnp.einsum("fks,fsa->fka", picked, all_coef, preferred_element_type=jnp.float32)
        half = jnp.where(column_ok[:, None, :], half, 0.0).astype(jnp.bfloat16)
        half = half.reshape(frag_total, chol_local, orb_rows, lno_width)

    received = lax.all_to_all(half, "orb", split_axis=0, concat_axis=0, tiled=True)

    with jax.named_scope("dressing"):
        weighted = (
            received.astype(jnp.float32) * weight_all.reshape(orb_size, 1, orb_rows, 1)
        ).astype(jnp.bfloat16)
        dressing_part = lax.dot_general(
            weighted.reshape(-1, lno_width),
            received.reshape(-1, lno_width),
            (((0,), (0,)), ((), ())),
            preferred_element_type=jnp.float32,
        )
        dressing = (lax.psum(dressing_part, "chol") * norm_factor).astype(jnp.bfloat16)

    with jax.named_scope("rotated"):
        rotated = jnp.einsum(
            "ora,ogrb->gab", own_w, received, preferred_element_type=jnp.float32
        ).astype(jnp.bfloat16)[:, None]
    return (rotated, dressing[None])


def solution(mesh):
    return jax.shard_map(
        per_device,
        mesh=mesh,
        in_specs=(P("chol", "orb", None), P("orb"), P("orb", None, None), P(), P(), P()),
        out_specs=(P("chol", "orb", None, None), P("orb", None, None)),
        check_vma=False,
    )
```

```python
import math

import jax
import jax.numpy as jnp
from jax import lax
from jax.sharding import PartitionSpec as P


def split_bf16(x):
    hi = lax.reduce_precision(x, exponent_bits=8, mantissa_bits=7)
    rest = x - hi
    mid = lax.reduce_precision(rest, exponent_bits=8, mantissa_bits=7)
    lo = rest - mid
    return jnp.stack([hi, mid, lo]).astype(jnp.bfloat16)


def join_bf16(parts):
    parts = parts.astype(jnp.float32)
    return (parts[0] + parts[1]) + parts[2]


def per_device(chol_vec, env_weight, lno_coef, domain, block_fill, lno_count):
    chol_local, orb_rows, orb_total = chol_vec.shape
    frag_total, slot_total = domain.shape
    group_count = block_fill.shape[1]
    group_width = slot_total // group_count
    lno_width = lno_coef.shape[2]
    chol_size = lax.axis_size("chol")
    orb_size = lax.axis_size("orb")
    my_index = lax.axis_index("orb")
    norm_factor = 1.0 / math.sqrt(chol_local * chol_size * orb_total)

    slot_index = jnp.arange(slot_total, dtype=jnp.int32)
    slot_ok = (slot_index % group_width)[None, :] < jnp.repeat(block_fill, group_width, axis=1)
    column_ok = jnp.arange(lno_width, dtype=jnp.int32)[None, :] < lno_count[:, None]

    with jax.named_scope("placement"):
        groups = domain.reshape(frag_total, group_count, group_width)
        group_block = groups[:, :, 0] // orb_rows
        block_ids = jnp.arange(orb_size, dtype=jnp.int32)
        sel = group_block[:, None, :] == block_ids[None, :, None]
        present = jnp.any(sel, axis=2)
        group_of_block = jnp.argmax(sel, axis=2).astype(jnp.int32)
        local = jnp.take_along_axis(groups, group_of_block[:, :, None], axis=1)
        local = local - block_ids[None, :, None] * orb_rows
        fill = jnp.take_along_axis(
            slot_ok.reshape(frag_total, group_count, group_width), group_of_block[:, :, None], axis=1
        ) & present[:, :, None]
        row_ids = jnp.arange(orb_rows, dtype=jnp.int32)
        onehot = ((local[:, :, None, :] == row_ids[None, None, :, None]) & fill[:, :, None, :]).astype(jnp.bfloat16)

    own_pick = lax.dynamic_index_in_dim(group_of_block, my_index, 0, keepdims=False)
    own_perm = jnp.take(lno_coef[0].reshape(group_count, group_width, lno_width), own_pick, axis=0)
    weight_rows = -(-3 * orb_rows // lno_width)
    pad_rows = -(-weight_rows // 8) * 8
    weight_parts = split_bf16(env_weight).reshape(-1)
    weight_parts = jnp.pad(weight_parts, (0, pad_rows * lno_width - weight_parts.shape[0]))
    payload = jnp.concatenate([lno_coef, weight_parts.reshape(1, pad_rows, lno_width)], axis=1)
    gathered = lax.all_gather(payload, "orb", axis=0, tiled=True)

    with jax.named_scope("pick_columns"):
        group_rows = groups - group_block[:, :, None] * orb_rows
        group_hot = (
            (group_rows[:, :, None, :] == row_ids[None, None, :, None])
            & slot_ok.reshape(frag_total, group_count, group_width)[:, :, None, :]
        ).astype(jnp.bfloat16)
        chol_blocks = chol_vec.reshape(chol_local * orb_rows, orb_size, orb_rows).transpose(1, 0, 2)
        chol_groups = jnp.take(chol_blocks, group_block, axis=0)
        picked = jnp.einsum(
            "fjkr,fjrc->fkjc", chol_groups, group_hot, preferred_element_type=jnp.float32
        ).astype(jnp.bfloat16).reshape(frag_total, chol_local * orb_rows, slot_total)

    with jax.named_scope("own_placement"):
        own_hot = lax.dynamic_index_in_dim(onehot, my_index, 0, keepdims=False)
        own_cols = lax.dynamic_index_in_dim(column_ok, my_index, 0, keepdims=False)
        own_w = jnp.einsum("orc,oca->ora", own_hot, own_perm, preferred_element_type=jnp.float32)
        own_w = jnp.where(own_cols[None, None, :], own_w, 0.0).astype(jnp.bfloat16)

    all_coef = gathered[:, :slot_total]
    weight_all = join_bf16(
        gathered[:, slot_total:]
        .reshape(orb_size, -1)[:, : 3 * orb_rows]
        .reshape(orb_size, 3, orb_rows)
        .transpose(1, 0, 2)
    )

    with jax.named_scope("half"):
        half = jnp.einsum("fsa,fks->fak", all_coef, picked, preferred_element_type=jnp.float32)
        half = jnp.where(column_ok[:, :, None], half, 0.0).astype(jnp.bfloat16)
        half = half.reshape(frag_total, lno_width, chol_local, orb_rows)

    received = lax.all_to_all(half, "orb", split_axis=0, concat_axis=0, tiled=True)

    with jax.named_scope("dressing"):
        weighted = (
            received.astype(jnp.float32) * weight_all.reshape(orb_size, 1, 1, orb_rows)
        ).astype(jnp.bfloat16)
        dressing_part = jnp.einsum(
            "oagr,obgr->ab", weighted, received, preferred_element_type=jnp.float32
        )
        dressing = (lax.psum(dressing_part, "chol") * norm_factor).astype(jnp.bfloat16)

    with jax.named_scope("rotated"):
        rotated = jnp.einsum(
            "ora,obgr->gab", own_w, received, preferred_element_type=jnp.float32
        ).astype(jnp.bfloat16)[:, None]
    return (rotated, dressing[None])


def solution(mesh):
    return jax.shard_map(
        per_device,
        mesh=mesh,
        in_specs=(P("chol", "orb", None), P("orb"), P("orb", None, None), P(), P(), P()),
        out_specs=(P("chol", "orb", None, None), P("orb", None, None)),
        check_vma=False,
    )
```

```python
import math

import jax
import jax.numpy as jnp
from jax import lax
from jax.sharding import PartitionSpec as P


def split_bf16(x):
    hi = lax.reduce_precision(x, exponent_bits=8, mantissa_bits=7)
    rest = x - hi
    mid = lax.reduce_precision(rest, exponent_bits=8, mantissa_bits=7)
    lo = rest - mid
    return jnp.stack([hi, mid, lo]).astype(jnp.bfloat16)


def join_bf16(parts):
    parts = parts.astype(jnp.float32)
    return (parts[0] + parts[1]) + parts[2]


def per_device(chol_vec, env_weight, lno_coef, domain, block_fill, lno_count):
    chol_local, orb_rows, orb_total = chol_vec.shape
    frag_total, slot_total = domain.shape
    group_count = block_fill.shape[1]
    group_width = slot_total // group_count
    lno_width = lno_coef.shape[2]
    chol_size = lax.axis_size("chol")
    orb_size = lax.axis_size("orb")
    my_index = lax.axis_index("orb")
    norm_factor = 1.0 / math.sqrt(chol_local * chol_size * orb_total)

    slot_index = jnp.arange(slot_total, dtype=jnp.int32)
    slot_ok = (slot_index % group_width)[None, :] < jnp.repeat(block_fill, group_width, axis=1)
    column_ok = jnp.arange(lno_width, dtype=jnp.int32)[None, :] < lno_count[:, None]

    with jax.named_scope("placement"):
        groups = domain.reshape(frag_total, group_count, group_width)
        group_block = groups[:, :, 0] // orb_rows
        block_ids = jnp.arange(orb_size, dtype=jnp.int32)
        sel = group_block[:, None, :] == block_ids[None, :, None]
        present = jnp.any(sel, axis=2)
        group_of_block = jnp.argmax(sel, axis=2).astype(jnp.int32)
        local = jnp.take_along_axis(groups, group_of_block[:, :, None], axis=1)
        local = local - block_ids[None, :, None] * orb_rows
        fill = jnp.take_along_axis(
            slot_ok.reshape(frag_total, group_count, group_width), group_of_block[:, :, None], axis=1
        ) & present[:, :, None]
        row_ids = jnp.arange(orb_rows, dtype=jnp.int32)
        onehot = ((local[:, :, None, :] == row_ids[None, None, :, None]) & fill[:, :, None, :]).astype(jnp.bfloat16)

    own_pick = lax.dynamic_index_in_dim(group_of_block, my_index, 0, keepdims=False)
    own_perm = jnp.take(lno_coef[0].reshape(group_count, group_width, lno_width), own_pick, axis=0)
    all_coef = lax.all_gather(lno_coef, "orb", axis=0, tiled=True)

    with jax.named_scope("pick_columns"):
        group_rows = groups - group_block[:, :, None] * orb_rows
        group_hot = (
            (group_rows[:, :, None, :] == row_ids[None, None, :, None])
            & slot_ok.reshape(frag_total, group_count, group_width)[:, :, None, :]
        ).astype(jnp.bfloat16)
        chol_blocks = chol_vec.reshape(chol_local * orb_rows, orb_size, orb_rows).transpose(1, 0, 2)
        chol_groups = jnp.take(chol_blocks, group_block, axis=0)
        picked = jnp.einsum(
            "fjkr,fjrc->fkjc", chol_groups, group_hot, preferred_element_type=jnp.float32
        ).astype(jnp.bfloat16).reshape(frag_total, chol_local * orb_rows, slot_total)

    with jax.named_scope("own_placement"):
        own_hot = lax.dynamic_index_in_dim(onehot, my_index, 0, keepdims=False)
        own_cols = lax.dynamic_index_in_dim(column_ok, my_index, 0, keepdims=False)
        own_w = jnp.einsum("orc,oca->ora", own_hot, own_perm, preferred_element_type=jnp.float32)
        own_w = jnp.where(own_cols[None, None, :], own_w, 0.0).astype(jnp.bfloat16)

    weight_all = lax.all_gather(env_weight, "orb", axis=0, tiled=False)
    weight_all, picked = lax.optimization_barrier((weight_all, picked))

    with jax.named_scope("half"):
        half = jnp.einsum("fks,fsa->fka", picked, all_coef, preferred_element_type=jnp.float32)
        half = jnp.where(column_ok[:, None, :], half, 0.0).astype(jnp.bfloat16)
        half = half.reshape(frag_total, chol_local, orb_rows, lno_width)

    received = lax.all_to_all(half, "orb", split_axis=0, concat_axis=0, tiled=True)

    with jax.named_scope("dressing"):
        weighted = (
            received.astype(jnp.float32) * weight_all.reshape(orb_size, 1, orb_rows, 1)
        ).astype(jnp.bfloat16)
        dressing_part = lax.dot_general(
            weighted.reshape(-1, lno_width),
            received.reshape(-1, lno_width),
            (((0,), (0,)), ((), ())),
            preferred_element_type=jnp.float32,
        )
        dressing = (lax.psum(dressing_part, "chol") * norm_factor).astype(jnp.bfloat16)

    with jax.named_scope("rotated"):
        rotated = jnp.einsum(
            "ora,ogrb->gab", own_w, received, preferred_element_type=jnp.float32
        ).astype(jnp.bfloat16)[:, None]
    return (rotated, dressing[None])


def solution(mesh):
    return jax.shard_map(
        per_device,
        mesh=mesh,
        in_specs=(P("chol", "orb", None), P("orb"), P("orb", None, None), P(), P(), P()),
        out_specs=(P("chol", "orb", None, None), P("orb", None, None)),
        check_vma=False,
    )
```

```python
import math

import jax
import jax.numpy as jnp
from jax import lax
from jax.sharding import Mesh, PartitionSpec as P
import numpy as np

ORB = ("orb_hi", "orb_lo")


def split_bf16(x):
    hi = lax.reduce_precision(x, exponent_bits=8, mantissa_bits=7)
    rest = x - hi
    mid = lax.reduce_precision(rest, exponent_bits=8, mantissa_bits=7)
    lo = rest - mid
    return jnp.stack([hi, mid, lo]).astype(jnp.bfloat16)


def join_bf16(parts):
    parts = parts.astype(jnp.float32)
    return (parts[0] + parts[1]) + parts[2]


def per_device(chol_vec, env_weight, lno_coef, domain, block_fill, lno_count):
    chol_local, orb_rows, orb_total = chol_vec.shape
    frag_total, slot_total = domain.shape
    group_count = block_fill.shape[1]
    group_width = slot_total // group_count
    lno_width = lno_coef.shape[2]
    chol_size = lax.axis_size("chol")
    hi_size = lax.axis_size("orb_hi")
    lo_size = lax.axis_size("orb_lo")
    orb_size = hi_size * lo_size
    my_index = lax.axis_index("orb_hi") * lo_size + lax.axis_index("orb_lo")
    positions = np.arange(orb_size)
    frag_of_pos = (positions % hi_size) * lo_size + positions // hi_size
    norm_factor = 1.0 / math.sqrt(chol_local * chol_size * orb_total)

    slot_index = jnp.arange(slot_total, dtype=jnp.int32)
    slot_ok = (slot_index % group_width)[None, :] < jnp.repeat(block_fill, group_width, axis=1)
    column_ok = jnp.arange(lno_width, dtype=jnp.int32)[None, :] < lno_count[:, None]

    with jax.named_scope("placement"):
        groups = domain.reshape(frag_total, group_count, group_width)
        group_block = groups[:, :, 0] // orb_rows
        block_ids = jnp.arange(orb_size, dtype=jnp.int32)
        sel = group_block[:, None, :] == block_ids[None, :, None]
        present = jnp.any(sel, axis=2)
        group_of_block = jnp.argmax(sel, axis=2).astype(jnp.int32)
        local = jnp.take_along_axis(groups, group_of_block[:, :, None], axis=1)
        local = local - block_ids[None, :, None] * orb_rows
        fill = jnp.take_along_axis(
            slot_ok.reshape(frag_total, group_count, group_width), group_of_block[:, :, None], axis=1
        ) & present[:, :, None]
        row_ids = jnp.arange(orb_rows, dtype=jnp.int32)
        onehot = ((local[:, :, None, :] == row_ids[None, None, :, None]) & fill[:, :, None, :]).astype(jnp.bfloat16)

    own_pick = lax.dynamic_index_in_dim(group_of_block, my_index, 0, keepdims=False)
    own_perm = jnp.take(lno_coef[0].reshape(group_count, group_width, lno_width), own_pick, axis=0)
    across = lax.all_gather(lno_coef, "orb_hi", axis=0, tiled=True)
    all_coef = lax.all_gather(across, "orb_lo", axis=0, tiled=True)

    with jax.named_scope("pick_columns"):
        groups_p = groups[frag_of_pos]
        block_p = group_block[frag_of_pos]
        group_rows = groups_p - block_p[:, :, None] * orb_rows
        group_hot = (
            (group_rows[:, :, None, :] == row_ids[None, None, :, None])
            & slot_ok.reshape(frag_total, group_count, group_width)[frag_of_pos][:, :, None, :]
        ).astype(jnp.bfloat16)
        chol_blocks = chol_vec.reshape(chol_local * orb_rows, orb_size, orb_rows).transpose(1, 0, 2)
        chol_groups = jnp.take(chol_blocks, block_p, axis=0)
        picked = jnp.einsum(
            "fjkr,fjrc->fkjc", chol_groups, group_hot, preferred_element_type=jnp.float32
        ).astype(jnp.bfloat16).reshape(frag_total, chol_local * orb_rows, slot_total)

    with jax.named_scope("own_placement"):
        own_hot = lax.dynamic_index_in_dim(onehot, my_index, 0, keepdims=False)
        own_cols = lax.dynamic_index_in_dim(column_ok, my_index, 0, keepdims=False)
        own_w = jnp.einsum("orc,oca->ora", own_hot, own_perm, preferred_element_type=jnp.float32)
        own_w = jnp.where(own_cols[None, None, :], own_w, 0.0).astype(jnp.bfloat16)[frag_of_pos]

    weight_all = lax.all_gather(env_weight, ("orb_lo", "orb_hi"), axis=0, tiled=False)
    weight_all, picked = lax.optimization_barrier((weight_all, picked))

    with jax.named_scope("half"):
        half = jnp.einsum("fks,fsa->fka", picked, all_coef, preferred_element_type=jnp.float32)
        half = jnp.where(column_ok[frag_of_pos][:, None, :], half, 0.0).astype(jnp.bfloat16)
        half = half.reshape(frag_total, chol_local, orb_rows, lno_width)

    received = lax.all_to_all(half, ("orb_lo", "orb_hi"), split_axis=0, concat_axis=0, tiled=True)

    with jax.named_scope("dressing"):
        weighted = (
            received.astype(jnp.float32) * weight_all.reshape(orb_size, 1, orb_rows, 1)
        ).astype(jnp.bfloat16)
        dressing_part = lax.dot_general(
            weighted.reshape(-1, lno_width),
            received.reshape(-1, lno_width),
            (((0,), (0,)), ((), ())),
            preferred_element_type=jnp.float32,
        )
        dressing = (lax.psum(dressing_part, "chol") * norm_factor).astype(jnp.bfloat16)

    with jax.named_scope("rotated"):
        rotated = jnp.einsum(
            "ora,ogrb->gab", own_w, received, preferred_element_type=jnp.float32
        ).astype(jnp.bfloat16)[:, None]
    return (rotated, dressing[None])


def solution(mesh):
    devices = mesh.devices
    lo = 2 if devices.shape[1] % 2 == 0 else 1
    fine = Mesh(devices.reshape(devices.shape[0], devices.shape[1] // lo, lo), ("chol",) + ORB)
    return jax.shard_map(
        per_device,
        mesh=fine,
        in_specs=(P("chol", ORB, None), P(ORB), P(ORB, None, None), P(), P(), P()),
        out_specs=(P("chol", ORB, None, None), P(ORB, None, None)),
        check_vma=False,
    )
```

```python
import math

import jax
import jax.numpy as jnp
from jax import lax
from jax.sharding import PartitionSpec as P


def split_bf16(x):
    hi = lax.reduce_precision(x, exponent_bits=8, mantissa_bits=7)
    rest = x - hi
    mid = lax.reduce_precision(rest, exponent_bits=8, mantissa_bits=7)
    lo = rest - mid
    return jnp.stack([hi, mid, lo]).astype(jnp.bfloat16)


def join_bf16(parts):
    parts = parts.astype(jnp.float32)
    return (parts[0] + parts[1]) + parts[2]


def per_device(chol_vec, env_weight, lno_coef, domain, block_fill, lno_count):
    chol_local, orb_rows, orb_total = chol_vec.shape
    frag_total, slot_total = domain.shape
    group_count = block_fill.shape[1]
    group_width = slot_total // group_count
    lno_width = lno_coef.shape[2]
    chol_size = lax.axis_size("chol")
    orb_size = lax.axis_size("orb")
    my_index = lax.axis_index("orb")
    norm_factor = 1.0 / math.sqrt(chol_local * chol_size * orb_total)

    slot_index = jnp.arange(slot_total, dtype=jnp.int32)
    slot_ok = (slot_index % group_width)[None, :] < jnp.repeat(block_fill, group_width, axis=1)
    column_ok = jnp.arange(lno_width, dtype=jnp.int32)[None, :] < lno_count[:, None]

    with jax.named_scope("placement"):
        groups = domain.reshape(frag_total, group_count, group_width)
        group_block = groups[:, :, 0] // orb_rows
        block_ids = jnp.arange(orb_size, dtype=jnp.int32)
        sel = group_block[:, None, :] == block_ids[None, :, None]
        present = jnp.any(sel, axis=2)
        group_of_block = jnp.argmax(sel, axis=2).astype(jnp.int32)
        local = jnp.take_along_axis(groups, group_of_block[:, :, None], axis=1)
        local = local - block_ids[None, :, None] * orb_rows
        fill = jnp.take_along_axis(
            slot_ok.reshape(frag_total, group_count, group_width), group_of_block[:, :, None], axis=1
        ) & present[:, :, None]
        row_ids = jnp.arange(orb_rows, dtype=jnp.int32)
        onehot = ((local[:, :, None, :] == row_ids[None, None, :, None]) & fill[:, :, None, :]).astype(jnp.bfloat16)

    own_pick = lax.dynamic_index_in_dim(group_of_block, my_index, 0, keepdims=False)
    own_perm = jnp.take(lno_coef[0].reshape(group_count, group_width, lno_width), own_pick, axis=0)
    split = (lno_width * 2 // 3) // 128 * 128
    gathered = lax.all_gather(lno_coef[:, :, :split], "orb", axis=0, tiled=True)
    rest = lno_coef[:, :, split:]
    spread = lax.all_to_all(
        jnp.broadcast_to(rest, (orb_size,) + rest.shape[1:]), "orb", split_axis=0, concat_axis=0, tiled=True
    )
    all_coef = jnp.concatenate([gathered, spread], axis=2)

    with jax.named_scope("pick_columns"):
        group_rows = groups - group_block[:, :, None] * orb_rows
        group_hot = (
            (group_rows[:, :, None, :] == row_ids[None, None, :, None])
            & slot_ok.reshape(frag_total, group_count, group_width)[:, :, None, :]
        ).astype(jnp.bfloat16)
        chol_blocks = chol_vec.reshape(chol_local * orb_rows, orb_size, orb_rows).transpose(1, 0, 2)
        chol_groups = jnp.take(chol_blocks, group_block, axis=0)
        picked = jnp.einsum(
            "fjkr,fjrc->fkjc", chol_groups, group_hot, preferred_element_type=jnp.float32
        ).astype(jnp.bfloat16).reshape(frag_total, chol_local * orb_rows, slot_total)

    with jax.named_scope("own_placement"):
        own_hot = lax.dynamic_index_in_dim(onehot, my_index, 0, keepdims=False)
        own_cols = lax.dynamic_index_in_dim(column_ok, my_index, 0, keepdims=False)
        own_w = jnp.einsum("orc,oca->ora", own_hot, own_perm, preferred_element_type=jnp.float32)
        own_w = jnp.where(own_cols[None, None, :], own_w, 0.0).astype(jnp.bfloat16)

    weight_all = lax.all_gather(env_weight, "orb", axis=0, tiled=False)
    weight_all, picked = lax.optimization_barrier((weight_all, picked))

    with jax.named_scope("half"):
        half = jnp.einsum("fks,fsa->fka", picked, all_coef, preferred_element_type=jnp.float32)
        half = jnp.where(column_ok[:, None, :], half, 0.0).astype(jnp.bfloat16)
        half = half.reshape(frag_total, chol_local, orb_rows, lno_width)

    received = lax.all_to_all(half, "orb", split_axis=0, concat_axis=0, tiled=True)

    with jax.named_scope("dressing"):
        weighted = (
            received.astype(jnp.float32) * weight_all.reshape(orb_size, 1, orb_rows, 1)
        ).astype(jnp.bfloat16)
        dressing_part = lax.dot_general(
            weighted.reshape(-1, lno_width),
            received.reshape(-1, lno_width),
            (((0,), (0,)), ((), ())),
            preferred_element_type=jnp.float32,
        )
        dressing = (lax.psum(dressing_part, "chol") * norm_factor).astype(jnp.bfloat16)

    with jax.named_scope("rotated"):
        rotated = jnp.einsum(
            "ora,ogrb->gab", own_w, received, preferred_element_type=jnp.float32
        ).astype(jnp.bfloat16)[:, None]
    return (rotated, dressing[None])


def solution(mesh):
    return jax.shard_map(
        per_device,
        mesh=mesh,
        in_specs=(P("chol", "orb", None), P("orb"), P("orb", None, None), P(), P(), P()),
        out_specs=(P("chol", "orb", None, None), P("orb", None, None)),
        check_vma=False,
    )
```

```python
import math

import jax
import jax.numpy as jnp
from jax import lax
from jax.sharding import PartitionSpec as P


def split_bf16(x):
    hi = lax.reduce_precision(x, exponent_bits=8, mantissa_bits=7)
    rest = x - hi
    mid = lax.reduce_precision(rest, exponent_bits=8, mantissa_bits=7)
    lo = rest - mid
    return jnp.stack([hi, mid, lo]).astype(jnp.bfloat16)


def join_bf16(parts):
    parts = parts.astype(jnp.float32)
    return (parts[0] + parts[1]) + parts[2]


def per_device(chol_vec, env_weight, lno_coef, domain, block_fill, lno_count):
    chol_local, orb_rows, orb_total = chol_vec.shape
    frag_total, slot_total = domain.shape
    group_count = block_fill.shape[1]
    group_width = slot_total // group_count
    lno_width = lno_coef.shape[2]
    chol_size = lax.axis_size("chol")
    orb_size = lax.axis_size("orb")
    my_index = lax.axis_index("orb")
    norm_factor = 1.0 / math.sqrt(chol_local * chol_size * orb_total)

    slot_index = jnp.arange(slot_total, dtype=jnp.int32)
    slot_ok = (slot_index % group_width)[None, :] < jnp.repeat(block_fill, group_width, axis=1)
    column_ok = jnp.arange(lno_width, dtype=jnp.int32)[None, :] < lno_count[:, None]

    with jax.named_scope("placement"):
        groups = domain.reshape(frag_total, group_count, group_width)
        group_block = groups[:, :, 0] // orb_rows
        block_ids = jnp.arange(orb_size, dtype=jnp.int32)
        sel = group_block[:, None, :] == block_ids[None, :, None]
        present = jnp.any(sel, axis=2)
        group_of_block = jnp.argmax(sel, axis=2).astype(jnp.int32)
        local = jnp.take_along_axis(groups, group_of_block[:, :, None], axis=1)
        local = local - block_ids[None, :, None] * orb_rows
        fill = jnp.take_along_axis(
            slot_ok.reshape(frag_total, group_count, group_width), group_of_block[:, :, None], axis=1
        ) & present[:, :, None]
        row_ids = jnp.arange(orb_rows, dtype=jnp.int32)
        onehot = ((local[:, :, None, :] == row_ids[None, None, :, None]) & fill[:, :, None, :]).astype(jnp.bfloat16)

    own_pick = lax.dynamic_index_in_dim(group_of_block, my_index, 0, keepdims=False)
    own_perm = jnp.take(lno_coef[0].reshape(group_count, group_width, lno_width), own_pick, axis=0)
    split = (lno_width * 2 // 3) // 128 * 128
    gathered = lax.all_gather(lno_coef[:, :, :split], "orb", axis=0, tiled=True)
    rest_width = lno_width - split
    weight_rows = -(-3 * orb_rows // rest_width)
    pad_rows = -(-weight_rows // 8) * 8
    weight_parts = split_bf16(env_weight).reshape(-1)
    weight_parts = jnp.pad(weight_parts, (0, pad_rows * rest_width - weight_parts.shape[0]))
    rest = jnp.concatenate(
        [lno_coef[:, :, split:], weight_parts.reshape(1, pad_rows, rest_width)], axis=1
    )
    spread = lax.all_to_all(
        jnp.broadcast_to(rest, (orb_size,) + rest.shape[1:]), "orb", split_axis=0, concat_axis=0, tiled=True
    )
    all_coef = jnp.concatenate([gathered, spread[:, :slot_total]], axis=2)
    weight_all = join_bf16(
        spread[:, slot_total:]
        .reshape(orb_size, -1)[:, : 3 * orb_rows]
        .reshape(orb_size, 3, orb_rows)
        .transpose(1, 0, 2)
    )

    with jax.named_scope("pick_columns"):
        group_rows = groups - group_block[:, :, None] * orb_rows
        group_hot = (
            (group_rows[:, :, None, :] == row_ids[None, None, :, None])
            & slot_ok.reshape(frag_total, group_count, group_width)[:, :, None, :]
        ).astype(jnp.bfloat16)
        chol_blocks = chol_vec.reshape(chol_local * orb_rows, orb_size, orb_rows).transpose(1, 0, 2)
        chol_groups = jnp.take(chol_blocks, group_block, axis=0)
        picked = jnp.einsum(
            "fjkr,fjrc->fkjc", chol_groups, group_hot, preferred_element_type=jnp.float32
        ).astype(jnp.bfloat16).reshape(frag_total, chol_local * orb_rows, slot_total)

    with jax.named_scope("own_placement"):
        own_hot = lax.dynamic_index_in_dim(onehot, my_index, 0, keepdims=False)
        own_cols = lax.dynamic_index_in_dim(column_ok, my_index, 0, keepdims=False)
        own_w = jnp.einsum("orc,oca->ora", own_hot, own_perm, preferred_element_type=jnp.float32)
        own_w = jnp.where(own_cols[None, None, :], own_w, 0.0).astype(jnp.bfloat16)


    with jax.named_scope("half"):
        half = jnp.einsum("fks,fsa->fka", picked, all_coef, preferred_element_type=jnp.float32)
        half = jnp.where(column_ok[:, None, :], half, 0.0).astype(jnp.bfloat16)
        half = half.reshape(frag_total, chol_local, orb_rows, lno_width)

    received = lax.all_to_all(half, "orb", split_axis=0, concat_axis=0, tiled=True)

    with jax.named_scope("dressing"):
        weighted = (
            received.astype(jnp.float32) * weight_all.reshape(orb_size, 1, orb_rows, 1)
        ).astype(jnp.bfloat16)
        dressing_part = lax.dot_general(
            weighted.reshape(-1, lno_width),
            received.reshape(-1, lno_width),
            (((0,), (0,)), ((), ())),
            preferred_element_type=jnp.float32,
        )
        dressing = (lax.psum(dressing_part, "chol") * norm_factor).astype(jnp.bfloat16)

    with jax.named_scope("rotated"):
        rotated = jnp.einsum(
            "ora,ogrb->gab", own_w, received, preferred_element_type=jnp.float32
        ).astype(jnp.bfloat16)[:, None]
    return (rotated, dressing[None])


def solution(mesh):
    return jax.shard_map(
        per_device,
        mesh=mesh,
        in_specs=(P("chol", "orb", None), P("orb"), P("orb", None, None), P(), P(), P()),
        out_specs=(P("chol", "orb", None, None), P("orb", None, None)),
        check_vma=False,
    )
```

```python
import math

import jax
import jax.numpy as jnp
from jax import lax
from jax.experimental.layout import Layout, with_layout_constraint
from jax.sharding import PartitionSpec as P


def split_bf16(x):
    hi = lax.reduce_precision(x, exponent_bits=8, mantissa_bits=7)
    rest = x - hi
    mid = lax.reduce_precision(rest, exponent_bits=8, mantissa_bits=7)
    lo = rest - mid
    return jnp.stack([hi, mid, lo]).astype(jnp.bfloat16)


def join_bf16(parts):
    parts = parts.astype(jnp.float32)
    return (parts[0] + parts[1]) + parts[2]


def per_device(chol_vec, env_weight, lno_coef, domain, block_fill, lno_count):
    chol_local, orb_rows, orb_total = chol_vec.shape
    frag_total, slot_total = domain.shape
    group_count = block_fill.shape[1]
    group_width = slot_total // group_count
    lno_width = lno_coef.shape[2]
    chol_size = lax.axis_size("chol")
    orb_size = lax.axis_size("orb")
    my_index = lax.axis_index("orb")
    norm_factor = 1.0 / math.sqrt(chol_local * chol_size * orb_total)

    slot_index = jnp.arange(slot_total, dtype=jnp.int32)
    slot_ok = (slot_index % group_width)[None, :] < jnp.repeat(block_fill, group_width, axis=1)
    column_ok = jnp.arange(lno_width, dtype=jnp.int32)[None, :] < lno_count[:, None]

    with jax.named_scope("placement"):
        groups = domain.reshape(frag_total, group_count, group_width)
        group_block = groups[:, :, 0] // orb_rows
        block_ids = jnp.arange(orb_size, dtype=jnp.int32)
        sel = group_block[:, None, :] == block_ids[None, :, None]
        present = jnp.any(sel, axis=2)
        group_of_block = jnp.argmax(sel, axis=2).astype(jnp.int32)
        local = jnp.take_along_axis(groups, group_of_block[:, :, None], axis=1)
        local = local - block_ids[None, :, None] * orb_rows
        fill = jnp.take_along_axis(
            slot_ok.reshape(frag_total, group_count, group_width), group_of_block[:, :, None], axis=1
        ) & present[:, :, None]
        row_ids = jnp.arange(orb_rows, dtype=jnp.int32)
        onehot = ((local[:, :, None, :] == row_ids[None, None, :, None]) & fill[:, :, None, :]).astype(jnp.bfloat16)

    own_pick = lax.dynamic_index_in_dim(group_of_block, my_index, 0, keepdims=False)
    own_perm = jnp.take(lno_coef[0].reshape(group_count, group_width, lno_width), own_pick, axis=0)
    all_coef = lax.all_gather(lno_coef, "orb", axis=0, tiled=True)

    with jax.named_scope("pick_columns"):
        group_rows = groups - group_block[:, :, None] * orb_rows
        group_hot = (
            (group_rows[:, :, None, :] == row_ids[None, None, :, None])
            & slot_ok.reshape(frag_total, group_count, group_width)[:, :, None, :]
        ).astype(jnp.bfloat16)
        chol_blocks = chol_vec.reshape(chol_local * orb_rows, orb_size, orb_rows).transpose(1, 0, 2)
        chol_groups = jnp.take(chol_blocks, group_block, axis=0)
        picked = jnp.einsum(
            "fjkr,fjrc->fkjc", chol_groups, group_hot, preferred_element_type=jnp.float32
        ).astype(jnp.bfloat16).reshape(frag_total, chol_local * orb_rows, slot_total)
        picked = with_layout_constraint(picked, Layout(major_to_minor=(0, 1, 2)))

    with jax.named_scope("own_placement"):
        own_hot = lax.dynamic_index_in_dim(onehot, my_index, 0, keepdims=False)
        own_cols = lax.dynamic_index_in_dim(column_ok, my_index, 0, keepdims=False)
        own_w = jnp.einsum("orc,oca->ora", own_hot, own_perm, preferred_element_type=jnp.float32)
        own_w = jnp.where(own_cols[None, None, :], own_w, 0.0).astype(jnp.bfloat16)

    weight_all = lax.all_gather(env_weight, "orb", axis=0, tiled=False)
    weight_all, picked = lax.optimization_barrier((weight_all, picked))

    with jax.named_scope("half"):
        half = jnp.einsum("fks,fsa->fka", picked, all_coef, preferred_element_type=jnp.float32)
        half = jnp.where(column_ok[:, None, :], half, 0.0).astype(jnp.bfloat16)
        half = half.reshape(frag_total, chol_local, orb_rows, lno_width)

    received = lax.all_to_all(half, "orb", split_axis=0, concat_axis=0, tiled=True)

    with jax.named_scope("dressing"):
        weighted = (
            received.astype(jnp.float32) * weight_all.reshape(orb_size, 1, orb_rows, 1)
        ).astype(jnp.bfloat16)
        dressing_part = lax.dot_general(
            weighted.reshape(-1, lno_width),
            received.reshape(-1, lno_width),
            (((0,), (0,)), ((), ())),
            preferred_element_type=jnp.float32,
        )
        dressing = (lax.psum(dressing_part, "chol") * norm_factor).astype(jnp.bfloat16)

    with jax.named_scope("rotated"):
        rotated = jnp.einsum(
            "ora,ogrb->gab", own_w, received, preferred_element_type=jnp.float32
        ).astype(jnp.bfloat16)[:, None]
    return (rotated, dressing[None])


def solution(mesh):
    return jax.shard_map(
        per_device,
        mesh=mesh,
        in_specs=(P("chol", "orb", None), P("orb"), P("orb", None, None), P(), P(), P()),
        out_specs=(P("chol", "orb", None, None), P("orb", None, None)),
        check_vma=False,
    )
```

```python
import math

import jax
import jax.numpy as jnp
from jax import lax
from jax.sharding import PartitionSpec as P


def split_bf16(x):
    hi = lax.reduce_precision(x, exponent_bits=8, mantissa_bits=7)
    rest = x - hi
    mid = lax.reduce_precision(rest, exponent_bits=8, mantissa_bits=7)
    lo = rest - mid
    return jnp.stack([hi, mid, lo]).astype(jnp.bfloat16)


def join_bf16(parts):
    parts = parts.astype(jnp.float32)
    return (parts[0] + parts[1]) + parts[2]


def per_device(chol_vec, env_weight, lno_coef, domain, block_fill, lno_count):
    chol_local, orb_rows, orb_total = chol_vec.shape
    frag_total, slot_total = domain.shape
    group_count = block_fill.shape[1]
    group_width = slot_total // group_count
    lno_width = lno_coef.shape[2]
    chol_size = lax.axis_size("chol")
    orb_size = lax.axis_size("orb")
    my_index = lax.axis_index("orb")
    norm_factor = 1.0 / math.sqrt(chol_local * chol_size * orb_total)

    slot_index = jnp.arange(slot_total, dtype=jnp.int32)
    slot_ok = (slot_index % group_width)[None, :] < jnp.repeat(block_fill, group_width, axis=1)
    column_ok = jnp.arange(lno_width, dtype=jnp.int32)[None, :] < lno_count[:, None]

    with jax.named_scope("placement"):
        groups = domain.reshape(frag_total, group_count, group_width)
        group_block = groups[:, :, 0] // orb_rows
        block_ids = jnp.arange(orb_size, dtype=jnp.int32)
        sel = group_block[:, None, :] == block_ids[None, :, None]
        present = jnp.any(sel, axis=2)
        group_of_block = jnp.argmax(sel, axis=2).astype(jnp.int32)
        local = jnp.take_along_axis(groups, group_of_block[:, :, None], axis=1)
        local = local - block_ids[None, :, None] * orb_rows
        fill = jnp.take_along_axis(
            slot_ok.reshape(frag_total, group_count, group_width), group_of_block[:, :, None], axis=1
        ) & present[:, :, None]
        row_ids = jnp.arange(orb_rows, dtype=jnp.int32)
        onehot = ((local[:, :, None, :] == row_ids[None, None, :, None]) & fill[:, :, None, :]).astype(jnp.bfloat16)

    own_pick = lax.dynamic_index_in_dim(group_of_block, my_index, 0, keepdims=False)
    own_perm = jnp.take(lno_coef[0].reshape(group_count, group_width, lno_width), own_pick, axis=0)
    all_coef = lax.all_gather(lno_coef, "orb", axis=0, tiled=True)

    with jax.named_scope("pick_columns"):
        group_rows = groups - group_block[:, :, None] * orb_rows
        group_hot = (
            (group_rows[:, :, None, :] == row_ids[None, None, :, None])
            & slot_ok.reshape(frag_total, group_count, group_width)[:, :, None, :]
        ).astype(jnp.bfloat16)
        chol_blocks = chol_vec.reshape(chol_local * orb_rows, orb_size, orb_rows).transpose(1, 0, 2)
        chol_groups = jnp.take(chol_blocks, group_block, axis=0)
        picked = jnp.einsum(
            "fjkr,fjrc->fkjc", chol_groups, group_hot, preferred_element_type=jnp.float32
        ).astype(jnp.bfloat16).reshape(frag_total, chol_local * orb_rows, slot_total)

    with jax.named_scope("own_placement"):
        own_hot = lax.dynamic_index_in_dim(onehot, my_index, 0, keepdims=False)
        own_cols = lax.dynamic_index_in_dim(column_ok, my_index, 0, keepdims=False)
        own_w = jnp.einsum("orc,oca->ora", own_hot, own_perm, preferred_element_type=jnp.float32)
        own_w = jnp.where(own_cols[None, None, :], own_w, 0.0).astype(jnp.bfloat16)

    weight_all = lax.all_gather(env_weight, "orb", axis=0, tiled=False)
    weight_all, picked = lax.optimization_barrier((weight_all, picked))

    split = chol_local // 2 if chol_local % 2 == 0 else chol_local
    parts = [(0, split), (split, chol_local)] if split < chol_local else [(0, chol_local)]
    dressing_part = None
    rot_parts = []
    for lo, hi in parts:
        width = hi - lo
        with jax.named_scope("half"):
            rows = picked[:, lo * orb_rows : hi * orb_rows]
            half = jnp.einsum("fks,fsa->fka", rows, all_coef, preferred_element_type=jnp.float32)
            half = jnp.where(column_ok[:, None, :], half, 0.0).astype(jnp.bfloat16)
            half = half.reshape(frag_total, width, orb_rows, lno_width)
        received = lax.all_to_all(half, "orb", split_axis=0, concat_axis=0, tiled=True)
        with jax.named_scope("dressing"):
            weighted = (
                received.astype(jnp.float32) * weight_all.reshape(orb_size, 1, orb_rows, 1)
            ).astype(jnp.bfloat16)
            term = lax.dot_general(
                weighted.reshape(-1, lno_width),
                received.reshape(-1, lno_width),
                (((0,), (0,)), ((), ())),
                preferred_element_type=jnp.float32,
            )
            dressing_part = term if dressing_part is None else dressing_part + term
        with jax.named_scope("rotated"):
            rot_parts.append(
                jnp.einsum("ora,ogrb->gab", own_w, received, preferred_element_type=jnp.float32).astype(
                    jnp.bfloat16
                )
            )
    with jax.named_scope("dressing"):
        dressing = (lax.psum(dressing_part, "chol") * norm_factor).astype(jnp.bfloat16)
    rotated = jnp.concatenate(rot_parts, axis=0)[:, None]
    return (rotated, dressing[None])


def solution(mesh):
    return jax.shard_map(
        per_device,
        mesh=mesh,
        in_specs=(P("chol", "orb", None), P("orb"), P("orb", None, None), P(), P(), P()),
        out_specs=(P("chol", "orb", None, None), P("orb", None, None)),
        check_vma=False,
    )
```

```python
import math

import jax
import jax.numpy as jnp
from jax import lax
from jax.sharding import PartitionSpec as P


def split_bf16(x):
    hi = lax.reduce_precision(x, exponent_bits=8, mantissa_bits=7)
    rest = x - hi
    mid = lax.reduce_precision(rest, exponent_bits=8, mantissa_bits=7)
    lo = rest - mid
    return jnp.stack([hi, mid, lo]).astype(jnp.bfloat16)


def join_bf16(parts):
    parts = parts.astype(jnp.float32)
    return (parts[0] + parts[1]) + parts[2]


def per_device(chol_vec, env_weight, lno_coef, domain, block_fill, lno_count):
    chol_local, orb_rows, orb_total = chol_vec.shape
    frag_total, slot_total = domain.shape
    group_count = block_fill.shape[1]
    group_width = slot_total // group_count
    lno_width = lno_coef.shape[2]
    chol_size = lax.axis_size("chol")
    orb_size = lax.axis_size("orb")
    my_index = lax.axis_index("orb")
    norm_factor = 1.0 / math.sqrt(chol_local * chol_size * orb_total)

    slot_index = jnp.arange(slot_total, dtype=jnp.int32)
    slot_ok = (slot_index % group_width)[None, :] < jnp.repeat(block_fill, group_width, axis=1)
    column_ok = jnp.arange(lno_width, dtype=jnp.int32)[None, :] < lno_count[:, None]

    with jax.named_scope("placement"):
        groups = domain.reshape(frag_total, group_count, group_width)
        group_block = groups[:, :, 0] // orb_rows
        block_ids = jnp.arange(orb_size, dtype=jnp.int32)
        sel = group_block[:, None, :] == block_ids[None, :, None]
        present = jnp.any(sel, axis=2)
        group_of_block = jnp.argmax(sel, axis=2).astype(jnp.int32)
        local = jnp.take_along_axis(groups, group_of_block[:, :, None], axis=1)
        local = local - block_ids[None, :, None] * orb_rows
        fill = jnp.take_along_axis(
            slot_ok.reshape(frag_total, group_count, group_width), group_of_block[:, :, None], axis=1
        ) & present[:, :, None]
        row_ids = jnp.arange(orb_rows, dtype=jnp.int32)
        onehot = ((local[:, :, None, :] == row_ids[None, None, :, None]) & fill[:, :, None, :]).astype(jnp.bfloat16)

    own_pick = lax.dynamic_index_in_dim(group_of_block, my_index, 0, keepdims=False)
    own_perm = jnp.take(lno_coef[0].reshape(group_count, group_width, lno_width), own_pick, axis=0)
    all_coef = lax.all_gather(lno_coef, "orb", axis=0, tiled=True)

    with jax.named_scope("pick_columns"):
        group_rows = groups - group_block[:, :, None] * orb_rows
        group_hot = (
            (group_rows[:, :, None, :] == row_ids[None, None, :, None])
            & slot_ok.reshape(frag_total, group_count, group_width)[:, :, None, :]
        ).astype(jnp.bfloat16)
        chol_blocks = chol_vec.reshape(chol_local * orb_rows, orb_size, orb_rows).transpose(1, 0, 2)
        chol_groups = jnp.take(chol_blocks, group_block, axis=0)
        picked = jnp.einsum(
            "fjkr,fjrc->fkjc", chol_groups, group_hot, preferred_element_type=jnp.float32
        ).astype(jnp.bfloat16).reshape(frag_total, chol_local * orb_rows, slot_total)

    with jax.named_scope("own_placement"):
        own_hot = lax.dynamic_index_in_dim(onehot, my_index, 0, keepdims=False)
        own_cols = lax.dynamic_index_in_dim(column_ok, my_index, 0, keepdims=False)
        own_w = jnp.einsum("orc,oca->ora", own_hot, own_perm, preferred_element_type=jnp.float32)
        own_w = jnp.where(own_cols[None, None, :], own_w, 0.0).astype(jnp.bfloat16)

    weight_all = lax.all_gather(env_weight, "orb", axis=0, tiled=False)
    weight_all, picked = lax.optimization_barrier((weight_all, picked))

    with jax.named_scope("half"):
        half = jnp.einsum("fks,fsa->fka", picked, all_coef, preferred_element_type=jnp.float32)
        half = jnp.where(column_ok[:, None, :], half, 0.0).astype(jnp.bfloat16)
        half = half.reshape(frag_total, chol_local, orb_rows, lno_width)

    received = lax.all_to_all(half, "orb", split_axis=0, concat_axis=0, tiled=True)

    with jax.named_scope("dressing"):
        weighted = (
            received.astype(jnp.float32) * weight_all.reshape(orb_size, 1, orb_rows, 1)
        ).astype(jnp.bfloat16)
        dressing_part = lax.dot_general(
            weighted.reshape(-1, lno_width),
            received.reshape(-1, lno_width),
            (((0,), (0,)), ((), ())),
            preferred_element_type=jnp.float32,
        ) * norm_factor
        dressing = lax.psum(dressing_part, "chol").astype(jnp.bfloat16)

    with jax.named_scope("rotated"):
        rotated = jnp.einsum(
            "ora,ogrb->gab", own_w, received, preferred_element_type=jnp.float32
        ).astype(jnp.bfloat16)[:, None]
    return (rotated, dressing[None])


def solution(mesh):
    return jax.shard_map(
        per_device,
        mesh=mesh,
        in_specs=(P("chol", "orb", None), P("orb"), P("orb", None, None), P(), P(), P()),
        out_specs=(P("chol", "orb", None, None), P("orb", None, None)),
        check_vma=False,
    )
```

```python
import math

import jax
import jax.numpy as jnp
from jax import lax
from jax.sharding import PartitionSpec as P


def split_bf16(x):
    hi = lax.reduce_precision(x, exponent_bits=8, mantissa_bits=7)
    rest = x - hi
    mid = lax.reduce_precision(rest, exponent_bits=8, mantissa_bits=7)
    lo = rest - mid
    return jnp.stack([hi, mid, lo]).astype(jnp.bfloat16)


def join_bf16(parts):
    parts = parts.astype(jnp.float32)
    return (parts[0] + parts[1]) + parts[2]


def per_device(chol_vec, env_weight, lno_coef, domain, block_fill, lno_count):
    chol_local, orb_rows, orb_total = chol_vec.shape
    frag_total, slot_total = domain.shape
    group_count = block_fill.shape[1]
    group_width = slot_total // group_count
    lno_width = lno_coef.shape[2]
    chol_size = lax.axis_size("chol")
    orb_size = lax.axis_size("orb")
    my_index = lax.axis_index("orb")
    norm_factor = 1.0 / math.sqrt(chol_local * chol_size * orb_total)

    slot_index = jnp.arange(slot_total, dtype=jnp.int32)
    slot_ok = (slot_index % group_width)[None, :] < jnp.repeat(block_fill, group_width, axis=1)
    column_ok = jnp.arange(lno_width, dtype=jnp.int32)[None, :] < lno_count[:, None]

    with jax.named_scope("placement"):
        groups = domain.reshape(frag_total, group_count, group_width)
        group_block = groups[:, :, 0] // orb_rows
        block_ids = jnp.arange(orb_size, dtype=jnp.int32)
        sel = group_block[:, None, :] == block_ids[None, :, None]
        present = jnp.any(sel, axis=2)
        group_of_block = jnp.argmax(sel, axis=2).astype(jnp.int32)
        local = jnp.take_along_axis(groups, group_of_block[:, :, None], axis=1)
        local = local - block_ids[None, :, None] * orb_rows
        fill = jnp.take_along_axis(
            slot_ok.reshape(frag_total, group_count, group_width), group_of_block[:, :, None], axis=1
        ) & present[:, :, None]
        row_ids = jnp.arange(orb_rows, dtype=jnp.int32)
        onehot = ((local[:, :, None, :] == row_ids[None, None, :, None]) & fill[:, :, None, :]).astype(jnp.bfloat16)

    own_pick = lax.dynamic_index_in_dim(group_of_block, my_index, 0, keepdims=False)
    own_perm = jnp.take(lno_coef[0].reshape(group_count, group_width, lno_width), own_pick, axis=0)
    all_coef = lax.all_gather(lno_coef, "orb", axis=0, tiled=True)

    with jax.named_scope("pick_columns"):
        group_rows = groups - group_block[:, :, None] * orb_rows
        group_hot = (
            (group_rows[:, :, None, :] == row_ids[None, None, :, None])
            & slot_ok.reshape(frag_total, group_count, group_width)[:, :, None, :]
        ).astype(jnp.bfloat16)
        chol_blocks = chol_vec.reshape(chol_local * orb_rows, orb_size, orb_rows).transpose(1, 0, 2)
        chol_groups = jnp.take(chol_blocks, group_block, axis=0)
        picked = jnp.einsum(
            "fjkr,fjrc->fkjc", chol_groups, group_hot, preferred_element_type=jnp.float32
        ).astype(jnp.bfloat16).reshape(frag_total, chol_local * orb_rows, slot_total)

    with jax.named_scope("own_placement"):
        own_hot = lax.dynamic_index_in_dim(onehot, my_index, 0, keepdims=False)
        own_cols = lax.dynamic_index_in_dim(column_ok, my_index, 0, keepdims=False)
        own_w = jnp.einsum("orc,oca->ora", own_hot, own_perm, preferred_element_type=jnp.float32)
        own_w = jnp.where(own_cols[None, None, :], own_w, 0.0).astype(jnp.bfloat16)

    weight_all = lax.all_gather(env_weight, "orb", axis=0, tiled=False)
    weight_all, picked = lax.optimization_barrier((weight_all, picked))

    with jax.named_scope("half"):
        half = jnp.einsum("fks,fsa->fka", picked, all_coef, preferred_element_type=jnp.float32)
        half = jnp.where(column_ok[:, None, :], half, 0.0).astype(jnp.bfloat16)
        half = half.reshape(frag_total, chol_local, orb_rows, lno_width)

    received = lax.all_to_all(half, "orb", split_axis=0, concat_axis=0, tiled=True)

    with jax.named_scope("dressing"):
        weighted = (
            received.astype(jnp.float32) * weight_all.reshape(orb_size, 1, orb_rows, 1)
        ).astype(jnp.bfloat16)
        dressing_part = lax.dot_general(
            weighted.reshape(-1, lno_width),
            received.reshape(-1, lno_width),
            (((0,), (0,)), ((), ())),
            preferred_element_type=jnp.float32,
        ) * norm_factor
        dressing = lax.psum(dressing_part, "chol").astype(jnp.bfloat16)

    with jax.named_scope("rotated"):
        rotated = jnp.einsum(
            "ogrb,ora->gab", received, own_w, preferred_element_type=jnp.float32
        ).astype(jnp.bfloat16)[:, None]
    return (rotated, dressing[None])


def solution(mesh):
    return jax.shard_map(
        per_device,
        mesh=mesh,
        in_specs=(P("chol", "orb", None), P("orb"), P("orb", None, None), P(), P(), P()),
        out_specs=(P("chol", "orb", None, None), P("orb", None, None)),
        check_vma=False,
    )
```
